256 devices in a mesh: rep: 32 (over x, y, core), tp: 8 (over z).
Axes of the slice: x: 4, y: 4, z: 8, core: 2. Of those that a mesh axis runs over, the one named last changes fastest.
Arguments:
- prompt_rows: bfloat16 [20480, 2048], P(('rep', 'tp')), may hold values from -6 to 6
- prompt_pieces: int32 [32, 640], P('rep'), may hold values from 0 to 9, never falling along the last dimension, each value on 1 to 320 neighbouring positions
- decode_rows: bfloat16 [1280, 2048], P('rep'), may hold values from -6 to 6
- request_ages: int32 [1280], P('rep'), may hold values from 2 to 127
- migrate_to: int32 [512, 1], P('rep'), may hold values from 0 to 31, as said below
- past_cache: bfloat16 [1280, 2, 128, 2048], P('rep', None, None, 'tp'), may hold values from -8 to 8
- norm_gain: float32 [2048], replicated, may hold values from 0.5 to 1.5
- norm_bias: float32 [2048], replicated, may hold values from -2 to 2
- qkv_weight: bfloat16 [3, 2048, 2048], P(None, None, 'tp'), may hold values from -0.125 to 0.125
- qkv_bias: float32 [3, 2048], P(None, 'tp'), may hold values from -4 to 4
- out_weight: bfloat16 [2048, 2048], P('tp'), may hold values from -0.125 to 0.125
- out_bias: float32 [2048], replicated, may hold values from -3 to 3
Outputs:
- prompt_out: bfloat16 [20480, 2048], P(('rep', 'tp'))
- prompt_cache: bfloat16 [2, 20480, 2048], P(None, 'rep', 'tp')
- kept_out: bfloat16 [768, 2048], P('rep')
- kept_cache: bfloat16 [768, 2, 128, 2048], P('rep', None, None, 'tp')
- moved_out: bfloat16 [1024, 2048], P('rep')
- moved_cache: bfloat16 [1024, 2, 128, 2048], P('rep', None, None, 'tp')
The draws below stay inside these ranges and needn't reach their ends.
Inputs may be any that keep to these rules, and one draw needn't show every extreme that they name: `migrate_to`: the 16 requests that leave one replica name 16 different target replicas, and one target replica is named by every replica. `prompt_pieces`: piece numbers never fall along a replica's prompt tokens; a piece has at most 320 tokens, and some piece exactly that many.
All inputs are finite; a program needn't handle non-finite values.
Results may differ from the reference program's by a relative error of at most 0.014.
Values may be sent and summed in bfloat16 or wider, within the bound.
No kernel may reach another device: no remote copies, remote signals or barrier semaphores. Data moves between devices by JAX's collectives and lax.ppermute only.
A program may use at most 128 MiB of HBM per device.

```python
import math
import jax
import jax.numpy as jnp
import numpy as np
from jax import lax

D = 2048
HEADS = 16
HEAD_DIM = 128
PROMPT_TOK = 640
KEEP = 24
CACHE_LEN = 128
CAP = 1
SLOTS = 32
OUT = 16
REQS = 40
N_REP = 32
N_TP = 8


def draw_migrate_to(key, part):
    favored = jax.random.randint(jax.random.fold_in(key, 11), (), 0, N_REP)
    replica_keys = jax.random.split(jax.random.fold_in(key, 12), N_REP)
    orders = jax.vmap(lambda one_key: jax.random.permutation(one_key, N_REP))(replica_keys)
    order_rank = jnp.where(orders == favored, -1, jnp.arange(N_REP)[None, :])
    picked = jnp.argsort(order_rank, axis=1, stable=True)
    chosen = jnp.take_along_axis(orders, picked, axis=1)[:, :OUT]
    return chosen.reshape(N_REP * OUT, 1).astype(jnp.int32)


def draw_qkv_bias(key, part):
    noise_field = 0.5 * jax.random.normal(jax.random.fold_in(key, 21), (3, D), jnp.float32)
    result = jnp.clip(noise_field, -3.0, 3.0)
    return result


def draw_past_cache(key, part):
    count = N_REP * REQS
    noise_field = jax.random.normal(jax.random.fold_in(key, 31), (count, 2, CACHE_LEN, D), jnp.float32)
    base_values = jnp.clip(noise_field, -6.0, 6.0)
    result = base_values
    return result.astype(jnp.bfloat16)


def plant(drawn, rng, low, high):
    longest = drawn.shape.index(max(drawn.shape))
    spots = []
    for shift in (0, 1):
        where = [jax.random.randint(jax.random.fold_in(rng, axis), (), 0, length) for axis, length in enumerate(drawn.shape)]
        where[longest] = (where[longest] + shift) % drawn.shape[longest]
        spots.append(tuple(where))
    return drawn.at[spots[0]].set(low).at[spots[1]].set(high)


def block_scale(stream_key, dims, cuts, smallest, top_value):
    gain, own = 1.0, jax.random.fold_in(stream_key, 6)
    for dim, parts in cuts:
        heights = jnp.exp(jax.random.uniform(jax.random.fold_in(own, dim), (parts,), jnp.float32, smallest / len(cuts), top_value / len(cuts)))
        gain = gain * jnp.repeat(heights, dims[dim] // parts).reshape([-1 if axis == dim else 1 for axis in range(len(dims))])
    return gain


def profile(count, total, most, skew):
    weights = [(1 << 20) // math.isqrt(rank ** skew) + 1 for rank in range(2, count + 1)]
    surplus, given = total - most - (count - 1), [1] * (count - 1)
    while surplus > 0:
        movable = [i for i in range(count - 1) if given[i] < most]
        mass, budget = sum([weights[i] for i in movable]), surplus
        for i in movable:
            extra = min(most - given[i], max(1, budget * weights[i] // mass), surplus)
            given[i] = given[i] + extra
            surplus = surplus - extra
    return np.array([most] + given)


def ragged(rng, number_of, total, most, slope):
    if number_of == 2:
        one = jax.random.randint(rng, (), max(1, total - most), min(most, total - 1) + 1)
        return jnp.stack([one, total - one])
    lengths = jnp.asarray(profile(number_of, total, most, slope), jnp.int32)
    pairs = (number_of - 1) // 2
    donor, sink = lengths[1:1 + 2 * pairs:2], lengths[2:2 + 2 * pairs:2]
    margin = jnp.minimum(donor - 1, most - sink)
    passed = jax.random.randint(jax.random.fold_in(rng, 1), (pairs,), 0, 1 << 20) % (margin + 1)
    lengths = lengths.at[1:1 + 2 * pairs:2].set(donor - passed).at[2:2 + 2 * pairs:2].set(sink + passed)
    return lengths[jax.random.permutation(jax.random.fold_in(rng, 2), number_of)]


def gaussian(own_key, shape, width, limit, cuts=(), held_as=jnp.bfloat16):
    array = jax.random.normal(own_key, shape, jnp.float32) * width
    if len(cuts) > 0:
        array = block_scale(own_key, shape, cuts, -0.22, 0.18) * array
    return jnp.clip(array, min=-limit, max=limit).astype(held_as)


def setup_inputs(seed: int = 0) -> dict:
    streams_of = jax.random.split(jax.random.key(seed), 13)
    return {
        "prompt_rows": gaussian(streams_of[0], (N_REP * PROMPT_TOK, D), 1.0, 6.0, ((0, 256),)),
        "prompt_pieces": jax.vmap(lambda own: jnp.searchsorted(jnp.cumsum(ragged(own, max(4, PROMPT_TOK // 64), PROMPT_TOK, PROMPT_TOK // 2, 2)), jnp.arange(PROMPT_TOK), side="right"))(jax.random.split(streams_of[1], N_REP)).reshape((N_REP, PROMPT_TOK)).astype(jnp.int32),
        "decode_rows": gaussian(streams_of[2], (N_REP * REQS, D), 1.0, 6.0, ((0, 32),)),
        "request_ages": plant(jax.random.randint(streams_of[3], (N_REP * REQS,), 2, CACHE_LEN), jax.random.fold_in(streams_of[3], 1), 2, CACHE_LEN - 1).astype(jnp.int32),
        "migrate_to": draw_migrate_to(jax.random.fold_in(streams_of[12], 71), 0),
        "past_cache": draw_past_cache(jax.random.fold_in(streams_of[12], 71), 0),
        "norm_gain": jnp.clip(1.0 + 0.1 * jax.random.normal(streams_of[6], (D,), jnp.float32), 0.5, 1.5),
        "norm_bias": gaussian(streams_of[7], (D,), 0.3, 2.0, (), jnp.float32),
        "qkv_weight": gaussian(streams_of[8], (3, D, D), D ** -0.5, 0.125, ((2, 8),)),
        "qkv_bias": draw_qkv_bias(jax.random.fold_in(streams_of[12], 71), 0),
        "out_weight": gaussian(streams_of[10], (D, D), D ** -0.5, 0.125, ((0, 8),)),
        "out_bias": gaussian(streams_of[11], (D,), 0.5, 3.0, (), jnp.float32),
    }


EPSILON = 1e-05

def layer_norm(values, norm_gain, norm_bias):
    wide = values.astype(jnp.float32)
    center = lax.optimization_barrier(jnp.mean(wide, axis=-1, keepdims=True))
    spread = lax.optimization_barrier(jnp.mean(jnp.square(wide - center), axis=-1, keepdims=True))
    scaled = (wide - center) * lax.rsqrt(spread + EPSILON)
    return (scaled * norm_gain.astype(jnp.float32) + norm_bias.astype(jnp.float32)).astype(jnp.bfloat16)

def project_all(normed, qkv_weight, qkv_bias):
    projected = jnp.einsum('rd,cde->cre', normed.astype(jnp.float32), qkv_weight.astype(jnp.float32))
    queries = (projected[0] + qkv_bias[0].astype(jnp.float32)).astype(jnp.bfloat16)
    key_rows = (projected[1] + qkv_bias[1].astype(jnp.float32)).astype(jnp.bfloat16)
    value_rows = (projected[2] + qkv_bias[2].astype(jnp.float32)).astype(jnp.bfloat16)
    return (queries, key_rows, value_rows)

def out_project(context, out_weight):
    count = context.shape[0]
    groups = context.astype(jnp.float32).reshape(count, N_TP, D // N_TP)
    weight = out_weight.astype(jnp.float32).reshape(N_TP, D // N_TP, D)
    partial_value = jnp.einsum('rge,ged->grd', groups, weight).astype(jnp.bfloat16)
    partial_value = lax.optimization_barrier(partial_value)
    return lax.optimization_barrier(jnp.sum(partial_value.astype(jnp.float32), axis=0))

def prompt_layer(inputs, norm_gain, norm_bias, qkv_weight, qkv_bias, out_weight, out_bias):
    rows, pieces = inputs
    normed = layer_norm(rows, norm_gain, norm_bias)
    queries, key_rows, value_rows = project_all(normed, qkv_weight, qkv_bias)
    length = rows.shape[0]
    head_q = queries.astype(jnp.float32).reshape(length, HEADS, HEAD_DIM)
    head_k = key_rows.astype(jnp.float32).reshape(length, HEADS, HEAD_DIM)
    head_v = value_rows.astype(jnp.float32).reshape(length, HEADS, HEAD_DIM)
    scores = jnp.einsum('qhe,khe->hqk', head_q, head_k) * HEAD_DIM ** (-0.5)
    position = jnp.arange(length)
    allowed = (pieces[:, None] == pieces[None, :]) & (position[None, :] <= position[:, None])
    scores = jnp.where(allowed[None], scores, -1e+30)
    highest = lax.optimization_barrier(jnp.max(scores, axis=-1, keepdims=True))
    weights = jnp.exp(scores - highest)
    probs = (weights / lax.optimization_barrier(jnp.sum(weights, axis=-1, keepdims=True))).astype(jnp.bfloat16)
    context = jnp.einsum('hqk,khe->qhe', probs.astype(jnp.float32), head_v)
    context = context.reshape(length, D).astype(jnp.bfloat16)
    attended = out_project(context, out_weight)
    output = (rows.astype(jnp.float32) + attended + out_bias.astype(jnp.float32)).astype(jnp.bfloat16)
    return (output, jnp.stack([key_rows, value_rows]))

def decode_layer(inputs, norm_gain, norm_bias, qkv_weight, qkv_bias, out_weight, out_bias):
    rows, cache, ages = inputs
    count = rows.shape[0]
    normed = layer_norm(rows, norm_gain, norm_bias)
    queries, key_new, value_new = project_all(normed, qkv_weight, qkv_bias)
    head_q = queries.astype(jnp.float32).reshape(count, HEADS, HEAD_DIM)
    old_keys = cache[:, 0].astype(jnp.float32).reshape(count, CACHE_LEN, HEADS, HEAD_DIM)
    old_values = cache[:, 1].astype(jnp.float32).reshape(count, CACHE_LEN, HEADS, HEAD_DIM)
    scale = HEAD_DIM ** (-0.5)
    scores = jnp.einsum('rhe,rlhe->rhl', head_q, old_keys) * scale
    own = lax.optimization_barrier(jnp.sum(head_q * key_new.astype(jnp.float32).reshape(count, HEADS, HEAD_DIM), axis=-1)) * scale
    live = jnp.arange(CACHE_LEN)[None, :] < ages[:, None]
    scores = jnp.where(live[:, None, :], scores, -1e+30)
    highest = jnp.maximum(lax.optimization_barrier(jnp.max(scores, axis=-1)), own)
    weights = jnp.exp(scores - highest[..., None])
    own_weight = jnp.exp(own - highest)
    total = lax.optimization_barrier(jnp.sum(weights, axis=-1)) + own_weight
    probs = (weights / total[..., None]).astype(jnp.bfloat16)
    own_prob = (own_weight / total).astype(jnp.bfloat16)
    context = jnp.einsum('rhl,rlhe->rhe', probs.astype(jnp.float32), old_values)
    context = context + own_prob.astype(jnp.float32)[..., None] * value_new.astype(jnp.float32).reshape(count, HEADS, HEAD_DIM)
    context = context.reshape(count, D).astype(jnp.bfloat16)
    attended = out_project(context, out_weight)
    output = (rows.astype(jnp.float32) + attended + out_bias.astype(jnp.float32)).astype(jnp.bfloat16)
    written = (jnp.arange(CACHE_LEN)[None, :] == ages[:, None])[:, :, None]
    new_keys = jnp.where(written, key_new[:, None, :], cache[:, 0])
    new_values = jnp.where(written, value_new[:, None, :], cache[:, 1])
    return (output, jnp.stack([new_keys, new_values], axis=1))

def reference(prompt_rows, prompt_pieces, decode_rows, request_ages, migrate_to, past_cache, norm_gain, norm_bias, qkv_weight, qkv_bias, out_weight, out_bias):
    params = (norm_gain, norm_bias, qkv_weight, qkv_bias, out_weight, out_bias)
    prompt_out, prompt_kv = lax.map(lambda item: prompt_layer(item, *params), (prompt_rows.reshape(N_REP, PROMPT_TOK, D), prompt_pieces))
    prompt_out = prompt_out.reshape(N_REP * PROMPT_TOK, D)
    prompt_cache = jnp.transpose(prompt_kv, (1, 0, 2, 3)).reshape(2, N_REP * PROMPT_TOK, D)
    decode_out, updated = lax.map(lambda item: decode_layer(item, *params), (decode_rows.reshape(N_REP, REQS, D), past_cache.reshape(N_REP, REQS, 2, CACHE_LEN, D), request_ages.reshape(N_REP, REQS)))
    kept_out = decode_out[:, :KEEP].reshape(N_REP * KEEP, D)
    kept_cache = updated[:, :KEEP].reshape(N_REP * KEEP, 2, CACHE_LEN, D)
    targets = migrate_to.reshape(N_REP, OUT)
    onehot = (targets[:, :, None] == jnp.arange(N_REP)[None, None, :]).astype(jnp.int32)
    earlier = jnp.cumsum(onehot, axis=1) - onehot
    rank = lax.optimization_barrier(jnp.sum(earlier * onehot, axis=-1)).astype(jnp.int32)
    slot = (targets * SLOTS + jnp.arange(N_REP)[:, None] * CAP + rank).reshape(-1).astype(jnp.int32)
    moved_out = jnp.zeros((N_REP * SLOTS, D), jnp.bfloat16).at[slot].set(decode_out[:, KEEP:].reshape(N_REP * OUT, D))
    moved_cache = jnp.zeros((N_REP * SLOTS, 2, CACHE_LEN, D), jnp.bfloat16).at[slot].set(updated[:, KEEP:].reshape(N_REP * OUT, 2, CACHE_LEN, D))
    return (prompt_out, prompt_cache, kept_out, kept_cache, moved_out, moved_cache)
```

```python
import jax
import jax.numpy as jnp
from jax import lax
from jax.sharding import PartitionSpec as P

HEAD_DIM = 128
CAP = 1


EPSILON = 1e-05


def layer_norm(values, norm_gain, norm_bias):
    wide = values.astype(jnp.float32)
    center = jnp.mean(wide, axis=-1, keepdims=True)
    spread = jnp.mean(jnp.square(wide - center), axis=-1, keepdims=True)
    scaled = (wide - center) * lax.rsqrt(spread + EPSILON)
    return (scaled * norm_gain + norm_bias).astype(jnp.bfloat16)


def decode_partial(
    rows, cache, live, position, norm_gain, norm_bias, qkv_weight, qkv_bias, out_weight
):
    count = rows.shape[0]
    width = qkv_weight.shape[2]
    heads_here = width // HEAD_DIM
    length = cache.shape[2]
    normed = layer_norm(rows, norm_gain, norm_bias)
    projected = jnp.einsum("rd,cde->cre", normed, qkv_weight, preferred_element_type=jnp.float32)
    queries = (projected[0] + qkv_bias[0]).astype(jnp.bfloat16).reshape(count, heads_here, HEAD_DIM)
    key_new = (projected[1] + qkv_bias[1]).astype(jnp.bfloat16)
    value_new = (projected[2] + qkv_bias[2]).astype(jnp.bfloat16)
    old_keys = cache[:, 0].reshape(count, length, heads_here, HEAD_DIM)
    old_values = cache[:, 1].reshape(count, length, heads_here, HEAD_DIM)
    scale = HEAD_DIM ** (-0.5)
    scores = (
        jnp.einsum("rhe,rlhe->rhl", queries, old_keys, preferred_element_type=jnp.float32) * scale
    )
    own = (
        jnp.sum(
            queries.astype(jnp.float32)
            * key_new.astype(jnp.float32).reshape(count, heads_here, HEAD_DIM),
            axis=-1,
        )
        * scale
    )
    scores = jnp.where(live[:, None, :], scores, -1e30)
    highest = jnp.maximum(jnp.max(scores, axis=-1), own)
    weights = jnp.exp(scores - highest[..., None])
    own_weight = jnp.exp(own - highest)
    total = jnp.sum(weights, axis=-1) + own_weight
    probs = (weights / total[..., None]).astype(jnp.bfloat16)
    own_prob = (own_weight / total).astype(jnp.bfloat16)
    context = jnp.einsum("rhl,rlhe->rhe", probs, old_values, preferred_element_type=jnp.float32)
    context = context + own_prob.astype(jnp.float32)[..., None] * value_new.astype(
        jnp.float32
    ).reshape(count, heads_here, HEAD_DIM)
    context = context.reshape(count, width).astype(jnp.bfloat16)
    partial_value = jnp.dot(context, out_weight, preferred_element_type=jnp.float32)
    written = (jnp.arange(length)[None, :] == position[:, None])[:, :, None]
    new_keys = jnp.where(written, key_new[:, None, :], cache[:, 0])
    new_values = jnp.where(written, value_new[:, None, :], cache[:, 1])
    return (partial_value, jnp.stack([new_keys, new_values], axis=1))


def reduce_over_tp(partial_value, rows, out_bias):
    n = lax.axis_size("tp")
    me = lax.axis_index("tp")
    count, model = rows.shape
    share = count // n
    pieces = partial_value.astype(jnp.bfloat16).reshape(n, share, model)
    rolled = jnp.take(pieces, (me + jnp.arange(n)) % n, axis=0)
    total = rolled[0].astype(jnp.float32)
    for shift in range(1, n):
        incoming = lax.ppermute(rolled[shift], "tp", [(i, (i + shift) % n) for i in range(n)])
        total = total + incoming.astype(jnp.float32)
    own_rows = lax.dynamic_slice_in_dim(rows, me * share, share, 0)
    own_out = (own_rows.astype(jnp.float32) + total + out_bias).astype(jnp.bfloat16)
    held = [own_out]
    for shift in range(1, n):
        held.append(lax.ppermute(own_out, "tp", [(i, (i + shift) % n) for i in range(n)]))
    stacked = jnp.stack(held)
    order = (me - jnp.arange(n)) % n
    return jnp.take(stacked, order, axis=0).reshape(count, model)


def on_device(
    prompt_rows,
    prompt_pieces,
    decode_rows,
    request_ages,
    migrate_to,
    past_cache,
    norm_gain,
    norm_bias,
    qkv_weight,
    qkv_bias,
    out_weight,
    out_bias,
):
    rep_count = lax.axis_size("rep")
    width = qkv_weight.shape[2]
    heads_here = width // HEAD_DIM
    length = past_cache.shape[2]
    leaving = migrate_to.shape[0]
    staying = decode_rows.shape[0] - leaving
    slot_count = rep_count * CAP
    targets = migrate_to[:, 0]
    onehot = (targets[:, None] == jnp.arange(rep_count)[None, :]).astype(jnp.float32)
    lower = (jnp.arange(leaving)[:, None] > jnp.arange(leaving)[None, :]).astype(jnp.float32)
    earlier = jnp.dot(lower, onehot)
    rank = jnp.sum(earlier * onehot, axis=1).astype(jnp.int32)
    slot = targets * CAP + rank
    placing = (jnp.arange(slot_count)[:, None] == slot[None, :]).astype(jnp.bfloat16)
    cells = jnp.arange(length)
    live = cells[None, :] < request_ages[:, None]
    partial_value, updated = decode_partial(
        decode_rows,
        past_cache,
        live,
        request_ages,
        norm_gain,
        norm_bias,
        qkv_weight,
        qkv_bias,
        out_weight,
    )
    send_cache = jnp.einsum(
        "so,oklh->sklh", placing, updated[staying:], preferred_element_type=jnp.float32
    ).astype(jnp.bfloat16)
    moved_cache = lax.all_to_all(send_cache, "rep", split_axis=0, concat_axis=0, tiled=True)
    normed = layer_norm(lax.all_gather(prompt_rows, "tp", axis=0, tiled=True), norm_gain, norm_bias)
    projected = jnp.einsum("rd,cde->cre", normed, qkv_weight, preferred_element_type=jnp.float32)
    total_rows = projected.shape[1]
    queries = (projected[0] + qkv_bias[0]).astype(jnp.bfloat16)
    key_rows = (projected[1] + qkv_bias[1]).astype(jnp.bfloat16)
    value_rows = (projected[2] + qkv_bias[2]).astype(jnp.bfloat16)
    head_q = queries.reshape(total_rows, heads_here, HEAD_DIM)
    head_k = key_rows.reshape(total_rows, heads_here, HEAD_DIM)
    head_v = value_rows.reshape(total_rows, heads_here, HEAD_DIM)
    scores = jnp.einsum(
        "qhe,khe->hqk", head_q, head_k, preferred_element_type=jnp.float32
    ) * HEAD_DIM ** (-0.5)
    pieces = prompt_pieces[0]
    position = jnp.arange(total_rows)
    allowed = (pieces[:, None] == pieces[None, :]) & (position[None, :] <= position[:, None])
    scores = jnp.where(allowed[None], scores, -1e30)
    highest = jnp.max(scores, axis=-1, keepdims=True)
    weights = jnp.exp(scores - highest)
    probs = (weights / jnp.sum(weights, axis=-1, keepdims=True)).astype(jnp.bfloat16)
    context = jnp.einsum("hqk,khe->qhe", probs, head_v, preferred_element_type=jnp.float32)
    context = context.reshape(total_rows, width).astype(jnp.bfloat16)
    decode_out = reduce_over_tp(partial_value, decode_rows, out_bias)
    context, moved_cache, decode_out = lax.optimization_barrier((context, moved_cache, decode_out))
    attended = lax.psum_scatter(
        jnp.dot(context, out_weight, preferred_element_type=jnp.float32).astype(jnp.bfloat16),
        "tp",
        scatter_dimension=0,
        tiled=True,
    ).astype(jnp.float32)
    prompt_out = (prompt_rows.astype(jnp.float32) + attended + out_bias).astype(jnp.bfloat16)
    prompt_cache = jnp.stack([key_rows, value_rows])
    kept_out = decode_out[:staying]
    kept_cache = updated[:staying]
    send_rows = jnp.dot(placing, decode_out[staying:], preferred_element_type=jnp.float32).astype(
        jnp.bfloat16
    )
    moved_out = lax.all_to_all(send_rows, "rep", split_axis=0, concat_axis=0, tiled=True)
    return (prompt_out, prompt_cache, kept_out, kept_cache, moved_out, moved_cache)


def solution(mesh):
    placed = (
        P(("rep", "tp"), None),
        P("rep", None),
        P("rep", None),
        P("rep"),
        P("rep", None),
        P("rep", None, None, "tp"),
        P(),
        P(),
        P(None, None, "tp"),
        P(None, "tp"),
        P("tp", None),
        P(),
    )
    return jax.shard_map(
        on_device,
        mesh=mesh,
        in_specs=placed,
        out_specs=(
            P(("rep", "tp"), None),
            P(None, "rep", "tp"),
            P("rep", None),
            P("rep", None, None, "tp"),
            P("rep", None),
            P("rep", None, None, "tp"),
        ),
        check_vma=False,
    )
```

```python
import jax
import jax.numpy as jnp
from jax import lax
from jax.sharding import PartitionSpec as P

HEAD_DIM = 128
CAP = 1


EPSILON = 1e-05


def layer_norm(values, norm_gain, norm_bias):
    wide = values.astype(jnp.float32)
    center = jnp.mean(wide, axis=-1, keepdims=True)
    spread = jnp.mean(jnp.square(wide - center), axis=-1, keepdims=True)
    scaled = (wide - center) * lax.rsqrt(spread + EPSILON)
    return (scaled * norm_gain + norm_bias).astype(jnp.bfloat16)


def decode_partial(rows, cache, ages, norm_gain, norm_bias, qkv_weight, qkv_bias, out_weight):
    count = rows.shape[0]
    width = qkv_weight.shape[2]
    heads_here = width // HEAD_DIM
    length = cache.shape[2]
    normed = layer_norm(rows, norm_gain, norm_bias)
    projected = jnp.einsum("rd,cde->cre", normed, qkv_weight, preferred_element_type=jnp.float32)
    queries = (projected[0] + qkv_bias[0]).astype(jnp.bfloat16)
    key_new = (projected[1] + qkv_bias[1]).astype(jnp.bfloat16)
    value_new = (projected[2] + qkv_bias[2]).astype(jnp.bfloat16)
    head_of_col = jnp.arange(width) // HEAD_DIM
    diag = jnp.arange(heads_here)[:, None] == head_of_col[None, :]
    q_blocks = jnp.where(diag[None], queries[:, None, :], jnp.zeros((), jnp.bfloat16))
    scale = HEAD_DIM ** (-0.5)
    scores = (
        jnp.einsum("rhc,rlc->rhl", q_blocks, cache[:, 0], preferred_element_type=jnp.float32)
        * scale
    )
    own = (
        jnp.sum(
            (queries.astype(jnp.float32) * key_new.astype(jnp.float32)).reshape(
                count, heads_here, HEAD_DIM
            ),
            axis=-1,
        )
        * scale
    )
    live = jnp.arange(length)[None, :] < ages[:, None]
    scores = jnp.where(live[:, None, :], scores, -1e30)
    highest = jnp.maximum(jnp.max(scores, axis=-1), own)
    weights = jnp.exp(scores - highest[..., None])
    own_weight = jnp.exp(own - highest)
    total = jnp.sum(weights, axis=-1) + own_weight
    probs = (weights / total[..., None]).astype(jnp.bfloat16)
    own_prob = (own_weight / total).astype(jnp.bfloat16)
    mixed = jnp.einsum("rhl,rlc->rhc", probs, cache[:, 1], preferred_element_type=jnp.float32)
    context = jnp.sum(jnp.where(diag[None], mixed, 0.0), axis=1)
    context = context + own_prob.astype(jnp.float32)[:, head_of_col] * value_new.astype(jnp.float32)
    context = context.astype(jnp.bfloat16)
    partial_value = jnp.dot(context, out_weight, preferred_element_type=jnp.float32)
    return partial_value, key_new, value_new


def updated_rows(cache, key_new, value_new, ages, picks):
    length = cache.shape[2]
    fresh = jnp.stack([key_new, value_new], axis=1)[picks]
    written = jnp.arange(length)[None, :] == ages[picks][:, None]
    return jnp.where(written[:, None, :, None], fresh[:, :, None, :], cache[picks])


def reduce_over_tp(partial_value, rows, out_bias):
    n = lax.axis_size("tp")
    me = lax.axis_index("tp")
    count, model = rows.shape
    rounds = n.bit_length() - 1
    held = partial_value.astype(jnp.bfloat16).astype(jnp.float32)
    chunk = jnp.zeros((), jnp.int32)
    for k in range(rounds):
        mask = 1 << k
        bit = (me >> k) & 1
        halves = held.reshape(2, held.shape[0] // 2, model)
        keep = lax.dynamic_index_in_dim(halves, bit, 0, keepdims=False)
        give = lax.dynamic_index_in_dim(halves, 1 - bit, 0, keepdims=False)
        got = lax.ppermute(give, "tp", [(i, i ^ mask) for i in range(n)])
        held = keep + got
        chunk = chunk * 2 + bit
    share = count // n
    own_rows = lax.dynamic_slice_in_dim(rows, chunk * share, share, 0)
    out = (own_rows.astype(jnp.float32) + held + out_bias).astype(jnp.bfloat16)
    for k in reversed(range(rounds)):
        mask = 1 << k
        bit = (me >> k) & 1
        got = lax.ppermute(out, "tp", [(i, i ^ mask) for i in range(n)])
        out = jnp.where(bit == 0, jnp.concatenate([out, got]), jnp.concatenate([got, out]))
    return out


def on_device(
    prompt_rows,
    prompt_pieces,
    decode_rows,
    request_ages,
    migrate_to,
    past_cache,
    norm_gain,
    norm_bias,
    qkv_weight,
    qkv_bias,
    out_weight,
    out_bias,
):
    rep_count = lax.axis_size("rep")
    width = qkv_weight.shape[2]
    heads_here = width // HEAD_DIM
    leaving = migrate_to.shape[0]
    staying = decode_rows.shape[0] - leaving
    targets = migrate_to[:, 0]
    match = targets[None, :] == jnp.arange(rep_count * CAP)[:, None]
    has = jnp.any(match, axis=1)
    picks = staying + jnp.sum(jnp.where(match, jnp.arange(leaving)[None, :], 0), axis=1)
    partial_value, key_new, value_new = decode_partial(
        decode_rows, past_cache, request_ages, norm_gain, norm_bias, qkv_weight, qkv_bias, out_weight
    )
    kept_cache = updated_rows(past_cache, key_new, value_new, request_ages, jnp.arange(staying))
    send_cache = jnp.where(
        has[:, None, None, None],
        updated_rows(past_cache, key_new, value_new, request_ages, picks),
        jnp.zeros((), jnp.bfloat16),
    )
    moved_cache = lax.all_to_all(send_cache, "rep", split_axis=0, concat_axis=0, tiled=True)
    decode_out = reduce_over_tp(partial_value, decode_rows, out_bias)
    normed = layer_norm(lax.all_gather(prompt_rows, "tp", axis=0, tiled=True), norm_gain, norm_bias)
    projected = jnp.einsum("rd,cde->cre", normed, qkv_weight, preferred_element_type=jnp.float32)
    total_rows = projected.shape[1]
    queries = (projected[0] + qkv_bias[0]).astype(jnp.bfloat16)
    key_rows = (projected[1] + qkv_bias[1]).astype(jnp.bfloat16)
    value_rows = (projected[2] + qkv_bias[2]).astype(jnp.bfloat16)
    head_q = queries.reshape(total_rows, heads_here, HEAD_DIM)
    head_k = key_rows.reshape(total_rows, heads_here, HEAD_DIM)
    head_v = value_rows.reshape(total_rows, heads_here, HEAD_DIM)
    scores = jnp.einsum(
        "qhe,khe->hqk", head_q, head_k, preferred_element_type=jnp.float32
    ) * HEAD_DIM ** (-0.5)
    pieces = prompt_pieces[0]
    position = jnp.arange(total_rows)
    allowed = (pieces[:, None] == pieces[None, :]) & (position[None, :] <= position[:, None])
    scores = jnp.where(allowed[None], scores, -1e30)
    highest = jnp.max(scores, axis=-1, keepdims=True)
    weights = jnp.exp(scores - highest)
    probs = (weights / jnp.sum(weights, axis=-1, keepdims=True)).astype(jnp.bfloat16)
    context = jnp.einsum("hqk,khe->qhe", probs, head_v, preferred_element_type=jnp.float32)
    context = context.reshape(total_rows, width).astype(jnp.bfloat16)
    context, moved_cache, decode_out = lax.optimization_barrier((context, moved_cache, decode_out))
    attended = lax.psum_scatter(
        jnp.dot(context, out_weight, preferred_element_type=jnp.float32).astype(jnp.bfloat16),
        "tp",
        scatter_dimension=0,
        tiled=True,
    ).astype(jnp.float32)
    prompt_out = (prompt_rows.astype(jnp.float32) + attended + out_bias).astype(jnp.bfloat16)
    prompt_cache = jnp.stack([key_rows, value_rows])
    kept_out = decode_out[:staying]
    send_rows = jnp.where(has[:, None], decode_out[picks], jnp.zeros((), jnp.bfloat16))
    moved_out = lax.all_to_all(send_rows, "rep", split_axis=0, concat_axis=0, tiled=True)
    return (prompt_out, prompt_cache, kept_out, kept_cache, moved_out, moved_cache)


def solution(mesh):
    placed = (
        P(("rep", "tp"), None),
        P("rep", None),
        P("rep", None),
        P("rep"),
        P("rep", None),
        P("rep", None, None, "tp"),
        P(),
        P(),
        P(None, None, "tp"),
        P(None, "tp"),
        P("tp", None),
        P(),
    )
    return jax.shard_map(
        on_device,
        mesh=mesh,
        in_specs=placed,
        out_specs=(
            P(("rep", "tp"), None),
            P(None, "rep", "tp"),
            P("rep", None),
            P("rep", None, None, "tp"),
            P("rep", None),
            P("rep", None, None, "tp"),
        ),
        check_vma=False,
    )
```

```python
import jax
import jax.numpy as jnp
from jax import lax
from jax.sharding import PartitionSpec as P

HEAD_DIM = 128
CAP = 1


EPSILON = 1e-05


def layer_norm(values, norm_gain, norm_bias):
    wide = values.astype(jnp.float32)
    center = jnp.mean(wide, axis=-1, keepdims=True)
    spread = jnp.mean(jnp.square(wide - center), axis=-1, keepdims=True)
    scaled = (wide - center) * lax.rsqrt(spread + EPSILON)
    return (scaled * norm_gain + norm_bias).astype(jnp.bfloat16)


def decode_partial(rows, cache, ages, norm_gain, norm_bias, qkv_weight, qkv_bias, out_weight):
    count = rows.shape[0]
    width = qkv_weight.shape[2]
    heads_here = width // HEAD_DIM
    length = cache.shape[2]
    normed = layer_norm(rows, norm_gain, norm_bias)
    projected = jnp.einsum("rd,cde->cre", normed, qkv_weight, preferred_element_type=jnp.float32)
    queries = (projected[0] + qkv_bias[0]).astype(jnp.bfloat16)
    key_new = (projected[1] + qkv_bias[1]).astype(jnp.bfloat16)
    value_new = (projected[2] + qkv_bias[2]).astype(jnp.bfloat16)
    head_of_col = jnp.arange(width) // HEAD_DIM
    diag = jnp.arange(heads_here)[:, None] == head_of_col[None, :]
    q_blocks = jnp.where(diag[None], queries[:, None, :], jnp.zeros((), jnp.bfloat16))
    scale = HEAD_DIM ** (-0.5)
    scores = (
        jnp.einsum("rhc,rlc->rhl", q_blocks, cache[:, 0], preferred_element_type=jnp.float32)
        * scale
    )
    own = (
        jnp.sum(
            (queries.astype(jnp.float32) * key_new.astype(jnp.float32)).reshape(
                count, heads_here, HEAD_DIM
            ),
            axis=-1,
        )
        * scale
    )
    live = jnp.arange(length)[None, :] < ages[:, None]
    scores = jnp.where(live[:, None, :], scores, -1e30)
    highest = jnp.maximum(jnp.max(scores, axis=-1), own)
    weights = jnp.exp(scores - highest[..., None])
    own_weight = jnp.exp(own - highest)
    total = jnp.sum(weights, axis=-1) + own_weight
    probs = (weights / total[..., None]).astype(jnp.bfloat16)
    own_prob = (own_weight / total).astype(jnp.bfloat16)
    mixed = jnp.einsum("rhl,rlc->rhc", probs, cache[:, 1], preferred_element_type=jnp.float32)
    context = jnp.sum(jnp.where(diag[None], mixed, 0.0), axis=1)
    context = context + own_prob.astype(jnp.float32)[:, head_of_col] * value_new.astype(jnp.float32)
    context = context.astype(jnp.bfloat16)
    partial_value = jnp.dot(context, out_weight, preferred_element_type=jnp.float32)
    return partial_value, key_new, value_new


def updated_rows(cache, key_new, value_new, ages, picks):
    length = cache.shape[2]
    fresh = jnp.stack([key_new, value_new], axis=1)[picks]
    written = jnp.arange(length)[None, :] == ages[picks][:, None]
    return jnp.where(written[:, None, :, None], fresh[:, :, None, :], cache[picks])


def reduce_over_tp(pieces, rows, out_bias):
    n = lax.axis_size("tp")
    count, model = rows.shape
    share = count // n
    arrived = lax.all_to_all(pieces, "tp", 0, 0, tiled=True)
    summed = jnp.sum(arrived.astype(jnp.float32), axis=0)
    own_rows = lax.dynamic_slice_in_dim(rows, lax.axis_index("tp") * share, share, 0)
    own_out = (own_rows.astype(jnp.float32) + summed + out_bias).astype(jnp.bfloat16)
    spread = jnp.broadcast_to(own_out[None], (n, share, model))
    return lax.all_to_all(spread, "tp", 0, 0, tiled=True).reshape(count, model)


def on_device(
    prompt_rows,
    prompt_pieces,
    decode_rows,
    request_ages,
    migrate_to,
    past_cache,
    norm_gain,
    norm_bias,
    qkv_weight,
    qkv_bias,
    out_weight,
    out_bias,
):
    rep_count = lax.axis_size("rep")
    width = qkv_weight.shape[2]
    heads_here = width // HEAD_DIM
    leaving = migrate_to.shape[0]
    staying = decode_rows.shape[0] - leaving
    targets = migrate_to[:, 0]
    match = targets[None, :] == jnp.arange(rep_count * CAP)[:, None]
    has = jnp.any(match, axis=1)
    picks = staying + jnp.sum(jnp.where(match, jnp.arange(leaving)[None, :], 0), axis=1)
    partial_value, key_new, value_new = decode_partial(
        decode_rows, past_cache, request_ages, norm_gain, norm_bias, qkv_weight, qkv_bias, out_weight
    )
    kept_cache = updated_rows(past_cache, key_new, value_new, request_ages, jnp.arange(staying))
    send_cache = jnp.where(
        has[:, None, None, None],
        updated_rows(past_cache, key_new, value_new, request_ages, picks),
        jnp.zeros((), jnp.bfloat16),
    )
    moved_cache = lax.all_to_all(send_cache, "rep", split_axis=0, concat_axis=0, tiled=True)
    tp_count = lax.axis_size("tp")
    decode_pieces = partial_value.astype(jnp.bfloat16).reshape(
        tp_count, decode_rows.shape[0] // tp_count, decode_rows.shape[1]
    )
    normed = layer_norm(lax.all_gather(prompt_rows, "tp", axis=0, tiled=True), norm_gain, norm_bias)
    projected = jnp.einsum("rd,cde->cre", normed, qkv_weight, preferred_element_type=jnp.float32)
    total_rows = projected.shape[1]
    queries = (projected[0] + qkv_bias[0]).astype(jnp.bfloat16)
    key_rows = (projected[1] + qkv_bias[1]).astype(jnp.bfloat16)
    value_rows = (projected[2] + qkv_bias[2]).astype(jnp.bfloat16)
    head_q = queries.reshape(total_rows, heads_here, HEAD_DIM)
    head_k = key_rows.reshape(total_rows, heads_here, HEAD_DIM)
    head_v = value_rows.reshape(total_rows, heads_here, HEAD_DIM)
    scores = jnp.einsum(
        "qhe,khe->hqk", head_q, head_k, preferred_element_type=jnp.float32
    ) * HEAD_DIM ** (-0.5)
    pieces = prompt_pieces[0]
    position = jnp.arange(total_rows)
    allowed = (pieces[:, None] == pieces[None, :]) & (position[None, :] <= position[:, None])
    scores = jnp.where(allowed[None], scores, -1e30)
    highest = jnp.max(scores, axis=-1, keepdims=True)
    weights = jnp.exp(scores - highest)
    probs = (weights / jnp.sum(weights, axis=-1, keepdims=True)).astype(jnp.bfloat16)
    context = jnp.einsum("hqk,khe->qhe", probs, head_v, preferred_element_type=jnp.float32)
    context = context.reshape(total_rows, width).astype(jnp.bfloat16)
    prompt_partial = jnp.dot(context, out_weight, preferred_element_type=jnp.float32).astype(
        jnp.bfloat16
    )
    prompt_partial, decode_pieces = lax.optimization_barrier((prompt_partial, decode_pieces))
    attended = lax.psum_scatter(prompt_partial, "tp", scatter_dimension=0, tiled=True).astype(
        jnp.float32
    )
    decode_pieces, moved_cache = lax.optimization_barrier((decode_pieces, moved_cache))
    decode_out = reduce_over_tp(decode_pieces, decode_rows, out_bias)
    prompt_out = (prompt_rows.astype(jnp.float32) + attended + out_bias).astype(jnp.bfloat16)
    prompt_cache = jnp.stack([key_rows, value_rows])
    kept_out = decode_out[:staying]
    send_rows = jnp.where(has[:, None], decode_out[picks], jnp.zeros((), jnp.bfloat16))
    moved_out = lax.all_to_all(send_rows, "rep", split_axis=0, concat_axis=0, tiled=True)
    return (prompt_out, prompt_cache, kept_out, kept_cache, moved_out, moved_cache)


def solution(mesh):
    placed = (
        P(("rep", "tp"), None),
        P("rep", None),
        P("rep", None),
        P("rep"),
        P("rep", None),
        P("rep", None, None, "tp"),
        P(),
        P(),
        P(None, None, "tp"),
        P(None, "tp"),
        P("tp", None),
        P(),
    )
    return jax.shard_map(
        on_device,
        mesh=mesh,
        in_specs=placed,
        out_specs=(
            P(("rep", "tp"), None),
            P(None, "rep", "tp"),
            P("rep", None),
            P("rep", None, None, "tp"),
            P("rep", None),
            P("rep", None, None, "tp"),
        ),
        check_vma=False,
    )
```

```python
import jax
import jax.numpy as jnp
from jax import lax
from jax.sharding import PartitionSpec as P

HEAD_DIM = 128
CAP = 1


EPSILON = 1e-05


def layer_norm(values, norm_gain, norm_bias):
    wide = values.astype(jnp.float32)
    center = jnp.mean(wide, axis=-1, keepdims=True)
    spread = jnp.mean(jnp.square(wide - center), axis=-1, keepdims=True)
    scaled = (wide - center) * lax.rsqrt(spread + EPSILON)
    return (scaled * norm_gain + norm_bias).astype(jnp.bfloat16)


def decode_partial(rows, cache, ages, norm_gain, norm_bias, qkv_weight, qkv_bias, out_weight):
    count = rows.shape[0]
    width = qkv_weight.shape[2]
    heads_here = width // HEAD_DIM
    length = cache.shape[2]
    normed = layer_norm(rows, norm_gain, norm_bias)
    projected = jnp.einsum("rd,cde->cre", normed, qkv_weight, preferred_element_type=jnp.float32)
    queries = (projected[0] + qkv_bias[0]).astype(jnp.bfloat16)
    key_new = (projected[1] + qkv_bias[1]).astype(jnp.bfloat16)
    value_new = (projected[2] + qkv_bias[2]).astype(jnp.bfloat16)
    head_of_col = jnp.arange(width) // HEAD_DIM
    diag = jnp.arange(heads_here)[:, None] == head_of_col[None, :]
    q_blocks = jnp.where(diag[None], queries[:, None, :], jnp.zeros((), jnp.bfloat16))
    scale = HEAD_DIM ** (-0.5)
    scores = (
        jnp.einsum("rhc,rlc->rhl", q_blocks, cache[:, 0], preferred_element_type=jnp.float32)
        * scale
    )
    own = (
        jnp.sum(
            (queries.astype(jnp.float32) * key_new.astype(jnp.float32)).reshape(
                count, heads_here, HEAD_DIM
            ),
            axis=-1,
        )
        * scale
    )
    live = jnp.arange(length)[None, :] < ages[:, None]
    scores = jnp.where(live[:, None, :], scores, -1e30)
    highest = jnp.maximum(jnp.max(scores, axis=-1), own)
    weights = jnp.exp(scores - highest[..., None])
    own_weight = jnp.exp(own - highest)
    total = jnp.sum(weights, axis=-1) + own_weight
    probs = (weights / total[..., None]).astype(jnp.bfloat16)
    own_prob = (own_weight / total).astype(jnp.bfloat16)
    mixed = jnp.einsum("rhl,rlc->rhc", probs, cache[:, 1], preferred_element_type=jnp.float32)
    context = jnp.sum(jnp.where(diag[None], mixed, 0.0), axis=1)
    context = context + own_prob.astype(jnp.float32)[:, head_of_col] * value_new.astype(jnp.float32)
    context = context.astype(jnp.bfloat16)
    partial_value = jnp.dot(context, out_weight, preferred_element_type=jnp.float32)
    return partial_value, key_new, value_new


def updated_rows(cache, key_new, value_new, ages, picks):
    length = cache.shape[2]
    fresh = jnp.stack([key_new, value_new], axis=1)[picks]
    written = jnp.arange(length)[None, :] == ages[picks][:, None]
    return jnp.where(written[:, None, :, None], fresh[:, :, None, :], cache[picks])


def scatter_over_tp(pieces, rows, out_bias):
    n = lax.axis_size("tp")
    me = lax.axis_index("tp")
    share = pieces.shape[1]
    rolled = jnp.take(pieces, (me + jnp.arange(n)) % n, axis=0)
    total = rolled[0].astype(jnp.float32)
    for shift in range(1, n):
        got = lax.ppermute(rolled[shift], "tp", [(i, (i + shift) % n) for i in range(n)])
        total = total + got.astype(jnp.float32)
    own_rows = lax.dynamic_slice_in_dim(rows, me * share, share, 0)
    return (own_rows.astype(jnp.float32) + total + out_bias).astype(jnp.bfloat16)


def gather_over_tp(own_out):
    n = lax.axis_size("tp")
    me = lax.axis_index("tp")
    held = [own_out]
    for shift in range(1, n):
        held.append(lax.ppermute(own_out, "tp", [(i, (i + shift) % n) for i in range(n)]))
    stacked = jnp.stack(held)
    return jnp.take(stacked, (me - jnp.arange(n)) % n, axis=0).reshape(-1, own_out.shape[1])


def on_device(
    prompt_rows,
    prompt_pieces,
    decode_rows,
    request_ages,
    migrate_to,
    past_cache,
    norm_gain,
    norm_bias,
    qkv_weight,
    qkv_bias,
    out_weight,
    out_bias,
):
    rep_count = lax.axis_size("rep")
    width = qkv_weight.shape[2]
    heads_here = width // HEAD_DIM
    leaving = migrate_to.shape[0]
    staying = decode_rows.shape[0] - leaving
    targets = migrate_to[:, 0]
    match = targets[None, :] == jnp.arange(rep_count * CAP)[:, None]
    has = jnp.any(match, axis=1)
    picks = staying + jnp.sum(jnp.where(match, jnp.arange(leaving)[None, :], 0), axis=1)
    partial_value, key_new, value_new = decode_partial(
        decode_rows, past_cache, request_ages, norm_gain, norm_bias, qkv_weight, qkv_bias, out_weight
    )
    kept_cache = updated_rows(past_cache, key_new, value_new, request_ages, jnp.arange(staying))
    send_cache = jnp.where(
        has[:, None, None, None],
        updated_rows(past_cache, key_new, value_new, request_ages, picks),
        jnp.zeros((), jnp.bfloat16),
    )
    moved_cache = lax.all_to_all(send_cache, "rep", split_axis=0, concat_axis=0, tiled=True)
    tp_count = lax.axis_size("tp")
    decode_pieces = partial_value.astype(jnp.bfloat16).reshape(
        tp_count, decode_rows.shape[0] // tp_count, decode_rows.shape[1]
    )
    own_out = scatter_over_tp(decode_pieces, decode_rows, out_bias)
    normed = lax.all_gather(layer_norm(prompt_rows, norm_gain, norm_bias), "tp", axis=0, tiled=True)
    projected = jnp.einsum("rd,cde->cre", normed, qkv_weight, preferred_element_type=jnp.float32)
    total_rows = projected.shape[1]
    queries = (projected[0] + qkv_bias[0]).astype(jnp.bfloat16)
    key_rows = (projected[1] + qkv_bias[1]).astype(jnp.bfloat16)
    value_rows = (projected[2] + qkv_bias[2]).astype(jnp.bfloat16)
    head_q = queries.reshape(total_rows, heads_here, HEAD_DIM)
    head_k = key_rows.reshape(total_rows, heads_here, HEAD_DIM)
    head_v = value_rows.reshape(total_rows, heads_here, HEAD_DIM)
    scores = jnp.einsum(
        "qhe,khe->hqk", head_q, head_k, preferred_element_type=jnp.float32
    ) * HEAD_DIM ** (-0.5)
    pieces = prompt_pieces[0]
    position = jnp.arange(total_rows)
    allowed = (pieces[:, None] == pieces[None, :]) & (position[None, :] <= position[:, None])
    scores = jnp.where(allowed[None], scores, -1e30)
    highest = jnp.max(scores, axis=-1, keepdims=True)
    weights = jnp.exp(scores - highest)
    probs = (weights / jnp.sum(weights, axis=-1, keepdims=True)).astype(jnp.bfloat16)
    context = jnp.einsum("hqk,khe->qhe", probs, head_v, preferred_element_type=jnp.float32)
    context = context.reshape(total_rows, width).astype(jnp.bfloat16)
    prompt_partial = jnp.dot(context, out_weight, preferred_element_type=jnp.float32).astype(
        jnp.bfloat16
    )
    prompt_partial, own_out, key_rows, value_rows = lax.optimization_barrier(
        (prompt_partial, own_out, key_rows, value_rows)
    )
    attended = lax.psum_scatter(prompt_partial, "tp", scatter_dimension=0, tiled=True).astype(
        jnp.float32
    )
    decode_out = gather_over_tp(own_out)
    prompt_out = (prompt_rows.astype(jnp.float32) + attended + out_bias).astype(jnp.bfloat16)
    prompt_cache = jnp.stack([key_rows, value_rows])
    kept_out = decode_out[:staying]
    send_rows = jnp.where(has[:, None], decode_out[picks], jnp.zeros((), jnp.bfloat16))
    send_rows, moved_cache = lax.optimization_barrier((send_rows, moved_cache))
    moved_out = lax.all_to_all(send_rows, "rep", split_axis=0, concat_axis=0, tiled=True)
    return (prompt_out, prompt_cache, kept_out, kept_cache, moved_out, moved_cache)


def solution(mesh):
    placed = (
        P(("rep", "tp"), None),
        P("rep", None),
        P("rep", None),
        P("rep"),
        P("rep", None),
        P("rep", None, None, "tp"),
        P(),
        P(),
        P(None, None, "tp"),
        P(None, "tp"),
        P("tp", None),
        P(),
    )
    return jax.shard_map(
        on_device,
        mesh=mesh,
        in_specs=placed,
        out_specs=(
            P(("rep", "tp"), None),
            P(None, "rep", "tp"),
            P("rep", None),
            P("rep", None, None, "tp"),
            P("rep", None),
            P("rep", None, None, "tp"),
        ),
        check_vma=False,
    )
```

```python
import jax
import jax.numpy as jnp
from jax import lax
from jax.sharding import PartitionSpec as P

HEAD_DIM = 128
CAP = 1


EPSILON = 1e-05


def layer_norm(values, norm_gain, norm_bias):
    wide = values.astype(jnp.float32)
    center = jnp.mean(wide, axis=-1, keepdims=True)
    spread = jnp.mean(jnp.square(wide - center), axis=-1, keepdims=True)
    scaled = (wide - center) * lax.rsqrt(spread + EPSILON)
    return (scaled * norm_gain + norm_bias).astype(jnp.bfloat16)


def decode_partial(rows, cache, ages, norm_gain, norm_bias, qkv_weight, qkv_bias, out_weight):
    count = rows.shape[0]
    width = qkv_weight.shape[2]
    heads_here = width // HEAD_DIM
    length = cache.shape[2]
    normed = layer_norm(rows, norm_gain, norm_bias)
    projected = jnp.einsum("rd,cde->cre", normed, qkv_weight, preferred_element_type=jnp.float32)
    queries = (projected[0] + qkv_bias[0]).astype(jnp.bfloat16)
    key_new = (projected[1] + qkv_bias[1]).astype(jnp.bfloat16)
    value_new = (projected[2] + qkv_bias[2]).astype(jnp.bfloat16)
    head_of_col = jnp.arange(width) // HEAD_DIM
    diag = jnp.arange(heads_here)[:, None] == head_of_col[None, :]
    q_blocks = jnp.where(diag[None], queries[:, None, :], jnp.zeros((), jnp.bfloat16))
    scale = HEAD_DIM ** (-0.5)
    scores = (
        jnp.einsum("rhc,rlc->rhl", q_blocks, cache[:, 0], preferred_element_type=jnp.float32)
        * scale
    )
    own = (
        jnp.sum(
            (queries.astype(jnp.float32) * key_new.astype(jnp.float32)).reshape(
                count, heads_here, HEAD_DIM
            ),
            axis=-1,
        )
        * scale
    )
    live = jnp.arange(length)[None, :] < ages[:, None]
    scores = jnp.where(live[:, None, :], scores, -1e30)
    highest = jnp.maximum(jnp.max(scores, axis=-1), own)
    weights = jnp.exp(scores - highest[..., None])
    own_weight = jnp.exp(own - highest)
    total = jnp.sum(weights, axis=-1) + own_weight
    probs = (weights / total[..., None]).astype(jnp.bfloat16)
    own_prob = (own_weight / total).astype(jnp.bfloat16)
    mixed = jnp.einsum("rhl,rlc->rhc", probs, cache[:, 1], preferred_element_type=jnp.float32)
    context = jnp.sum(jnp.where(diag[None], mixed, 0.0), axis=1)
    context = context + own_prob.astype(jnp.float32)[:, head_of_col] * value_new.astype(jnp.float32)
    context = context.astype(jnp.bfloat16)
    partial_value = jnp.dot(context, out_weight, preferred_element_type=jnp.float32)
    return partial_value, key_new, value_new


def updated_rows(cache, key_new, value_new, ages, picks):
    length = cache.shape[2]
    fresh = jnp.stack([key_new, value_new], axis=1)[picks]
    written = jnp.arange(length)[None, :] == ages[picks][:, None]
    return jnp.where(written[:, None, :, None], fresh[:, :, None, :], cache[picks])


def scatter_over_tp(pieces, rows, out_bias):
    n = lax.axis_size("tp")
    me = lax.axis_index("tp")
    share = pieces.shape[1]
    rolled = jnp.take(pieces, (me + jnp.arange(n)) % n, axis=0)
    total = rolled[0].astype(jnp.float32)
    for shift in range(1, n):
        got = lax.ppermute(rolled[shift], "tp", [(i, (i + shift) % n) for i in range(n)])
        total = total + got.astype(jnp.float32)
    own_rows = lax.dynamic_slice_in_dim(rows, me * share, share, 0)
    return (own_rows.astype(jnp.float32) + total + out_bias).astype(jnp.bfloat16)


def gather_over_tp(own_out):
    n = lax.axis_size("tp")
    me = lax.axis_index("tp")
    held = [own_out]
    for shift in range(1, n):
        held.append(lax.ppermute(own_out, "tp", [(i, (i + shift) % n) for i in range(n)]))
    stacked = jnp.stack(held)
    return jnp.take(stacked, (me - jnp.arange(n)) % n, axis=0).reshape(-1, own_out.shape[1])


def on_device(
    prompt_rows,
    prompt_pieces,
    decode_rows,
    request_ages,
    migrate_to,
    past_cache,
    norm_gain,
    norm_bias,
    qkv_weight,
    qkv_bias,
    out_weight,
    out_bias,
):
    rep_count = lax.axis_size("rep")
    width = qkv_weight.shape[2]
    heads_here = width // HEAD_DIM
    leaving = migrate_to.shape[0]
    staying = decode_rows.shape[0] - leaving
    targets = migrate_to[:, 0]
    match = targets[None, :] == jnp.arange(rep_count * CAP)[:, None]
    has = jnp.any(match, axis=1)
    picks = staying + jnp.sum(jnp.where(match, jnp.arange(leaving)[None, :], 0), axis=1)
    partial_value, key_new, value_new = decode_partial(
        decode_rows, past_cache, request_ages, norm_gain, norm_bias, qkv_weight, qkv_bias, out_weight
    )
    send_cache = jnp.where(
        has[:, None, None, None],
        updated_rows(past_cache, key_new, value_new, request_ages, picks),
        jnp.zeros((), jnp.bfloat16),
    )
    moved_cache = lax.all_to_all(send_cache, "rep", split_axis=0, concat_axis=0, tiled=True)
    tp_count = lax.axis_size("tp")
    decode_pieces = partial_value.astype(jnp.bfloat16).reshape(
        tp_count, decode_rows.shape[0] // tp_count, decode_rows.shape[1]
    )
    own_out = scatter_over_tp(decode_pieces, decode_rows, out_bias)
    normed = lax.all_gather(layer_norm(prompt_rows, norm_gain, norm_bias), "tp", axis=0, tiled=True)
    projected = jnp.einsum("rd,cde->cre", normed, qkv_weight, preferred_element_type=jnp.float32)
    total_rows = projected.shape[1]
    queries = (projected[0] + qkv_bias[0]).astype(jnp.bfloat16)
    key_rows = (projected[1] + qkv_bias[1]).astype(jnp.bfloat16)
    value_rows = (projected[2] + qkv_bias[2]).astype(jnp.bfloat16)
    head_q = queries.reshape(total_rows, heads_here, HEAD_DIM)
    head_k = key_rows.reshape(total_rows, heads_here, HEAD_DIM)
    head_v = value_rows.reshape(total_rows, heads_here, HEAD_DIM)
    scores = jnp.einsum(
        "qhe,khe->hqk", head_q, head_k, preferred_element_type=jnp.float32
    ) * HEAD_DIM ** (-0.5)
    pieces = prompt_pieces[0]
    position = jnp.arange(total_rows)
    allowed = (pieces[:, None] == pieces[None, :]) & (position[None, :] <= position[:, None])
    scores = jnp.where(allowed[None], scores, -1e30)
    highest = jnp.max(scores, axis=-1, keepdims=True)
    weights = jnp.exp(scores - highest)
    probs = (weights / jnp.sum(weights, axis=-1, keepdims=True)).astype(jnp.bfloat16)
    context = jnp.einsum("hqk,khe->qhe", probs, head_v, preferred_element_type=jnp.float32)
    context = context.reshape(total_rows, width).astype(jnp.bfloat16)
    prompt_partial = jnp.dot(context, out_weight, preferred_element_type=jnp.float32).astype(
        jnp.bfloat16
    )
    prompt_partial, own_out, key_rows, value_rows, key_new, value_new = lax.optimization_barrier(
        (prompt_partial, own_out, key_rows, value_rows, key_new, value_new)
    )
    kept_cache = updated_rows(past_cache, key_new, value_new, request_ages, jnp.arange(staying))
    attended = lax.psum_scatter(prompt_partial, "tp", scatter_dimension=0, tiled=True).astype(
        jnp.float32
    )
    decode_out = gather_over_tp(own_out)
    prompt_out = (prompt_rows.astype(jnp.float32) + attended + out_bias).astype(jnp.bfloat16)
    prompt_cache = jnp.stack([key_rows, value_rows])
    kept_out = decode_out[:staying]
    send_rows = jnp.where(has[:, None], decode_out[picks], jnp.zeros((), jnp.bfloat16))
    send_rows, moved_cache = lax.optimization_barrier((send_rows, moved_cache))
    moved_out = lax.all_to_all(send_rows, "rep", split_axis=0, concat_axis=0, tiled=True)
    return (prompt_out, prompt_cache, kept_out, kept_cache, moved_out, moved_cache)


def solution(mesh):
    placed = (
        P(("rep", "tp"), None),
        P("rep", None),
        P("rep", None),
        P("rep"),
        P("rep", None),
        P("rep", None, None, "tp"),
        P(),
        P(),
        P(None, None, "tp"),
        P(None, "tp"),
        P("tp", None),
        P(),
    )
    return jax.shard_map(
        on_device,
        mesh=mesh,
        in_specs=placed,
        out_specs=(
            P(("rep", "tp"), None),
            P(None, "rep", "tp"),
            P("rep", None),
            P("rep", None, None, "tp"),
            P("rep", None),
            P("rep", None, None, "tp"),
        ),
        check_vma=False,
    )
```

```python
import jax
import jax.numpy as jnp
from jax import lax
from jax.sharding import PartitionSpec as P

HEAD_DIM = 128
CAP = 1


EPSILON = 1e-05


def layer_norm(values, norm_gain, norm_bias):
    wide = values.astype(jnp.float32)
    center = jnp.mean(wide, axis=-1, keepdims=True)
    spread = jnp.mean(jnp.square(wide - center), axis=-1, keepdims=True)
    scaled = (wide - center) * lax.rsqrt(spread + EPSILON)
    return (scaled * norm_gain + norm_bias).astype(jnp.bfloat16)


def decode_partial(rows, cache, ages, norm_gain, norm_bias, qkv_weight, qkv_bias, out_weight):
    count = rows.shape[0]
    width = qkv_weight.shape[2]
    heads_here = width // HEAD_DIM
    length = cache.shape[2]
    normed = layer_norm(rows, norm_gain, norm_bias)
    projected = jnp.einsum("rd,cde->cre", normed, qkv_weight, preferred_element_type=jnp.float32)
    queries = (projected[0] + qkv_bias[0]).astype(jnp.bfloat16)
    key_new = (projected[1] + qkv_bias[1]).astype(jnp.bfloat16)
    value_new = (projected[2] + qkv_bias[2]).astype(jnp.bfloat16)
    head_of_col = jnp.arange(width) // HEAD_DIM
    diag = jnp.arange(heads_here)[:, None] == head_of_col[None, :]
    q_blocks = jnp.where(diag[None], queries[:, None, :], jnp.zeros((), jnp.bfloat16))
    scale = HEAD_DIM ** (-0.5)
    scores = (
        jnp.einsum("rhc,rlc->rhl", q_blocks, cache[:, 0], preferred_element_type=jnp.float32)
        * scale
    )
    own = (
        jnp.sum(
            (queries.astype(jnp.float32) * key_new.astype(jnp.float32)).reshape(
                count, heads_here, HEAD_DIM
            ),
            axis=-1,
        )
        * scale
    )
    live = jnp.arange(length)[None, :] < ages[:, None]
    scores = jnp.where(live[:, None, :], scores, -1e30)
    highest = jnp.maximum(jnp.max(scores, axis=-1), own)
    weights = jnp.exp(scores - highest[..., None])
    own_weight = jnp.exp(own - highest)
    total = jnp.sum(weights, axis=-1) + own_weight
    probs = (weights / total[..., None]).astype(jnp.bfloat16)
    own_prob = (own_weight / total).astype(jnp.bfloat16)
    mixed = jnp.einsum("rhl,rlc->rhc", probs, cache[:, 1], preferred_element_type=jnp.float32)
    context = jnp.sum(jnp.where(diag[None], mixed, 0.0), axis=1)
    context = context + own_prob.astype(jnp.float32)[:, head_of_col] * value_new.astype(jnp.float32)
    context = context.astype(jnp.bfloat16)
    partial_value = jnp.dot(context, out_weight, preferred_element_type=jnp.float32)
    return partial_value, key_new, value_new


def updated_rows(cache, key_new, value_new, ages, picks):
    length = cache.shape[2]
    fresh = jnp.stack([key_new, value_new], axis=1)[picks]
    written = jnp.arange(length)[None, :] == ages[picks][:, None]
    return jnp.where(written[:, None, :, None], fresh[:, :, None, :], cache[picks])


def scatter_over_tp(pieces, rows, out_bias):
    n = lax.axis_size("tp")
    me = lax.axis_index("tp")
    share = pieces.shape[1]
    rolled = jnp.take(pieces, (me + jnp.arange(n)) % n, axis=0)
    total = rolled[0].astype(jnp.float32)
    for shift in range(1, n):
        got = lax.ppermute(rolled[shift], "tp", [(i, (i + shift) % n) for i in range(n)])
        total = total + got.astype(jnp.float32)
    own_rows = lax.dynamic_slice_in_dim(rows, me * share, share, 0)
    return (own_rows.astype(jnp.float32) + total + out_bias).astype(jnp.bfloat16)


def gather_over_tp(own_out):
    n = lax.axis_size("tp")
    me = lax.axis_index("tp")
    held = [own_out]
    for shift in range(1, n):
        held.append(lax.ppermute(own_out, "tp", [(i, (i + shift) % n) for i in range(n)]))
    stacked = jnp.stack(held)
    return jnp.take(stacked, (me - jnp.arange(n)) % n, axis=0).reshape(-1, own_out.shape[1])


def on_device(
    prompt_rows,
    prompt_pieces,
    decode_rows,
    request_ages,
    migrate_to,
    past_cache,
    norm_gain,
    norm_bias,
    qkv_weight,
    qkv_bias,
    out_weight,
    out_bias,
):
    rep_count = lax.axis_size("rep")
    width = qkv_weight.shape[2]
    heads_here = width // HEAD_DIM
    leaving = migrate_to.shape[0]
    staying = decode_rows.shape[0] - leaving
    targets = migrate_to[:, 0]
    match = targets[None, :] == jnp.arange(rep_count * CAP)[:, None]
    has = jnp.any(match, axis=1)
    picks = staying + jnp.sum(jnp.where(match, jnp.arange(leaving)[None, :], 0), axis=1)
    partial_value, key_new, value_new = decode_partial(
        decode_rows, past_cache, request_ages, norm_gain, norm_bias, qkv_weight, qkv_bias, out_weight
    )
    send_cache = jnp.where(
        has[:, None, None, None],
        updated_rows(past_cache, key_new, value_new, request_ages, picks),
        jnp.zeros((), jnp.bfloat16),
    )
    moved_cache = lax.all_to_all(send_cache, "rep", split_axis=0, concat_axis=0, tiled=True)
    tp_count = lax.axis_size("tp")
    decode_pieces = partial_value.astype(jnp.bfloat16).reshape(
        tp_count, decode_rows.shape[0] // tp_count, decode_rows.shape[1]
    )
    own_out = scatter_over_tp(decode_pieces, decode_rows, out_bias)
    normed = lax.all_gather(layer_norm(prompt_rows, norm_gain, norm_bias), "tp", axis=0, tiled=True)
    model = qkv_weight.shape[1]
    split_weight = qkv_weight.reshape(3, model, heads_here, HEAD_DIM)
    split_bias = qkv_bias.reshape(3, heads_here, 1, HEAD_DIM)
    projected = jnp.einsum(
        "rd,cdhe->chre", normed, split_weight, preferred_element_type=jnp.float32
    )
    total_rows = projected.shape[2]
    head_q = (projected[0] + split_bias[0]).astype(jnp.bfloat16)
    head_k = (projected[1] + split_bias[1]).astype(jnp.bfloat16)
    head_v = (projected[2] + split_bias[2]).astype(jnp.bfloat16)
    scores = jnp.einsum(
        "hqe,hke->hqk", head_q, head_k, preferred_element_type=jnp.float32
    ) * HEAD_DIM ** (-0.5)
    pieces = prompt_pieces[0]
    position = jnp.arange(total_rows)
    allowed = (pieces[:, None] == pieces[None, :]) & (position[None, :] <= position[:, None])
    scores = jnp.where(allowed[None], scores, -1e30)
    highest = jnp.max(scores, axis=-1, keepdims=True)
    weights = jnp.exp(scores - highest)
    probs = (weights / jnp.sum(weights, axis=-1, keepdims=True)).astype(jnp.bfloat16)
    context = jnp.einsum("hqk,hke->qhe", probs, head_v, preferred_element_type=jnp.float32)
    context = context.reshape(total_rows, width).astype(jnp.bfloat16)
    key_rows = jnp.transpose(head_k, (1, 0, 2)).reshape(total_rows, width)
    value_rows = jnp.transpose(head_v, (1, 0, 2)).reshape(total_rows, width)
    prompt_partial = jnp.dot(context, out_weight, preferred_element_type=jnp.float32).astype(
        jnp.bfloat16
    )
    prompt_partial, own_out, key_rows, value_rows, key_new, value_new = lax.optimization_barrier(
        (prompt_partial, own_out, key_rows, value_rows, key_new, value_new)
    )
    written = (jnp.arange(past_cache.shape[2])[None, :] == request_ages[:staying, None])
    fresh = jnp.stack([key_new[:staying], value_new[:staying]], axis=1)
    kept_cache = jnp.where(
        written[:, None, :, None], fresh[:, :, None, :], past_cache[:staying]
    )
    attended = lax.psum_scatter(prompt_partial, "tp", scatter_dimension=0, tiled=True).astype(
        jnp.float32
    )
    decode_out = gather_over_tp(own_out)
    prompt_out = (prompt_rows.astype(jnp.float32) + attended + out_bias).astype(jnp.bfloat16)
    prompt_cache = jnp.stack([key_rows, value_rows])
    kept_out = decode_out[:staying]
    send_rows = jnp.where(has[:, None], decode_out[picks], jnp.zeros((), jnp.bfloat16))
    send_rows, moved_cache = lax.optimization_barrier((send_rows, moved_cache))
    moved_out = lax.all_to_all(send_rows, "rep", split_axis=0, concat_axis=0, tiled=True)
    return (prompt_out, prompt_cache, kept_out, kept_cache, moved_out, moved_cache)


def solution(mesh):
    placed = (
        P(("rep", "tp"), None),
        P("rep", None),
        P("rep", None),
        P("rep"),
        P("rep", None),
        P("rep", None, None, "tp"),
        P(),
        P(),
        P(None, None, "tp"),
        P(None, "tp"),
        P("tp", None),
        P(),
    )
    return jax.shard_map(
        on_device,
        mesh=mesh,
        in_specs=placed,
        out_specs=(
            P(("rep", "tp"), None),
            P(None, "rep", "tp"),
            P("rep", None),
            P("rep", None, None, "tp"),
            P("rep", None),
            P("rep", None, None, "tp"),
        ),
        check_vma=False,
    )
```

```python
import jax
import jax.numpy as jnp
from jax import lax
from jax.sharding import PartitionSpec as P

HEAD_DIM = 128
CAP = 1


EPSILON = 1e-05


def layer_norm(values, norm_gain, norm_bias):
    wide = values.astype(jnp.float32)
    center = jnp.mean(wide, axis=-1, keepdims=True)
    spread = jnp.mean(jnp.square(wide - center), axis=-1, keepdims=True)
    scaled = (wide - center) * lax.rsqrt(spread + EPSILON)
    return (scaled * norm_gain + norm_bias).astype(jnp.bfloat16)


def decode_partial(rows, cache, ages, norm_gain, norm_bias, qkv_weight, qkv_bias, out_weight):
    count = rows.shape[0]
    width = qkv_weight.shape[2]
    heads_here = width // HEAD_DIM
    length = cache.shape[2]
    normed = layer_norm(rows, norm_gain, norm_bias)
    projected = jnp.einsum("rd,cde->cre", normed, qkv_weight, preferred_element_type=jnp.float32)
    queries = (projected[0] + qkv_bias[0]).astype(jnp.bfloat16)
    key_new = (projected[1] + qkv_bias[1]).astype(jnp.bfloat16)
    value_new = (projected[2] + qkv_bias[2]).astype(jnp.bfloat16)
    head_of_col = jnp.arange(width) // HEAD_DIM
    diag = jnp.arange(heads_here)[:, None] == head_of_col[None, :]
    q_blocks = jnp.where(diag[None], queries[:, None, :], jnp.zeros((), jnp.bfloat16))
    scale = HEAD_DIM ** (-0.5)
    scores = (
        jnp.einsum("rhc,rlc->rhl", q_blocks, cache[:, 0], preferred_element_type=jnp.float32)
        * scale
    )
    own = (
        jnp.sum(
            (queries.astype(jnp.float32) * key_new.astype(jnp.float32)).reshape(
                count, heads_here, HEAD_DIM
            ),
            axis=-1,
        )
        * scale
    )
    live = jnp.arange(length)[None, :] < ages[:, None]
    scores = jnp.where(live[:, None, :], scores, -1e30)
    highest = jnp.maximum(jnp.max(scores, axis=-1), own)
    weights = jnp.exp(scores - highest[..., None])
    own_weight = jnp.exp(own - highest)
    total = jnp.sum(weights, axis=-1) + own_weight
    probs = (weights / total[..., None]).astype(jnp.bfloat16)
    own_prob = (own_weight / total).astype(jnp.bfloat16)
    mixed = jnp.einsum("rhl,rlc->rhc", probs, cache[:, 1], preferred_element_type=jnp.float32)
    context = jnp.sum(jnp.where(diag[None], mixed, 0.0), axis=1)
    context = context + own_prob.astype(jnp.float32)[:, head_of_col] * value_new.astype(jnp.float32)
    context = context.astype(jnp.bfloat16)
    partial_value = jnp.dot(context, out_weight, preferred_element_type=jnp.float32)
    return partial_value, key_new, value_new


def updated_rows(cache, key_new, value_new, ages, picks):
    length = cache.shape[2]
    fresh = jnp.stack([key_new, value_new], axis=1)[picks]
    written = jnp.arange(length)[None, :] == ages[picks][:, None]
    return jnp.where(written[:, None, :, None], fresh[:, :, None, :], cache[picks])


def scatter_over_tp(pieces, rows, out_bias):
    n = lax.axis_size("tp")
    me = lax.axis_index("tp")
    share = pieces.shape[1]
    rolled = jnp.take(pieces, (me + jnp.arange(n)) % n, axis=0)
    total = rolled[0].astype(jnp.float32)
    for shift in range(1, n):
        got = lax.ppermute(rolled[shift], "tp", [(i, (i + shift) % n) for i in range(n)])
        total = total + got.astype(jnp.float32)
    own_rows = lax.dynamic_slice_in_dim(rows, me * share, share, 0)
    return (own_rows.astype(jnp.float32) + total + out_bias).astype(jnp.bfloat16)


def gather_over_tp(own_out):
    n = lax.axis_size("tp")
    me = lax.axis_index("tp")
    held = [own_out]
    for shift in range(1, n):
        held.append(lax.ppermute(own_out, "tp", [(i, (i + shift) % n) for i in range(n)]))
    stacked = jnp.stack(held)
    return jnp.take(stacked, (me - jnp.arange(n)) % n, axis=0).reshape(-1, own_out.shape[1])


def on_device(
    prompt_rows,
    prompt_pieces,
    decode_rows,
    request_ages,
    migrate_to,
    past_cache,
    norm_gain,
    norm_bias,
    qkv_weight,
    qkv_bias,
    out_weight,
    out_bias,
):
    rep_count = lax.axis_size("rep")
    width = qkv_weight.shape[2]
    heads_here = width // HEAD_DIM
    leaving = migrate_to.shape[0]
    staying = decode_rows.shape[0] - leaving
    targets = migrate_to[:, 0]
    match = targets[None, :] == jnp.arange(rep_count * CAP)[:, None]
    has = jnp.any(match, axis=1)
    picks = staying + jnp.sum(jnp.where(match, jnp.arange(leaving)[None, :], 0), axis=1)
    partial_value, key_new, value_new = decode_partial(
        decode_rows, past_cache, request_ages, norm_gain, norm_bias, qkv_weight, qkv_bias, out_weight
    )
    send_cache = jnp.where(
        has[:, None, None, None],
        updated_rows(past_cache, key_new, value_new, request_ages, picks),
        jnp.zeros((), jnp.bfloat16),
    )
    send_cache, partial_value = lax.optimization_barrier((send_cache, partial_value))
    moved_cache = lax.all_to_all(send_cache, "rep", split_axis=0, concat_axis=0, tiled=True)
    tp_count = lax.axis_size("tp")
    decode_pieces = partial_value.astype(jnp.bfloat16).reshape(
        tp_count, decode_rows.shape[0] // tp_count, decode_rows.shape[1]
    )
    own_out = scatter_over_tp(decode_pieces, decode_rows, out_bias)
    normed = lax.all_gather(layer_norm(prompt_rows, norm_gain, norm_bias), "tp", axis=0, tiled=True)
    projected = jnp.einsum("rd,cde->cre", normed, qkv_weight, preferred_element_type=jnp.float32)
    total_rows = projected.shape[1]
    queries = (projected[0] + qkv_bias[0]).astype(jnp.bfloat16)
    key_rows = (projected[1] + qkv_bias[1]).astype(jnp.bfloat16)
    value_rows = (projected[2] + qkv_bias[2]).astype(jnp.bfloat16)
    diag = jnp.arange(heads_here)[:, None] == (jnp.arange(width) // HEAD_DIM)[None, :]
    q_blocks = jnp.where(diag[:, None, :], queries[None], jnp.zeros((), jnp.bfloat16))
    scores = jnp.einsum(
        "hqc,kc->hqk", q_blocks, key_rows, preferred_element_type=jnp.float32
    ) * HEAD_DIM ** (-0.5)
    pieces = prompt_pieces[0]
    position = jnp.arange(total_rows)
    allowed = (pieces[:, None] == pieces[None, :]) & (position[None, :] <= position[:, None])
    scores = jnp.where(allowed[None], scores, -1e30)
    highest = jnp.max(scores, axis=-1, keepdims=True)
    weights = jnp.exp(scores - highest)
    probs = (weights / jnp.sum(weights, axis=-1, keepdims=True)).astype(jnp.bfloat16)
    mixed = jnp.einsum("hqk,kc->hqc", probs, value_rows, preferred_element_type=jnp.float32)
    context = jnp.sum(jnp.where(diag[:, None, :], mixed, 0.0), axis=0).astype(jnp.bfloat16)
    prompt_partial = jnp.dot(context, out_weight, preferred_element_type=jnp.float32).astype(
        jnp.bfloat16
    )
    prompt_partial, own_out, key_rows, value_rows, key_new, value_new = lax.optimization_barrier(
        (prompt_partial, own_out, key_rows, value_rows, key_new, value_new)
    )
    written = (jnp.arange(past_cache.shape[2])[None, :] == request_ages[:staying, None])
    fresh = jnp.stack([key_new[:staying], value_new[:staying]], axis=1)
    kept_cache = jnp.where(
        written[:, None, :, None], fresh[:, :, None, :], past_cache[:staying]
    )
    attended = lax.psum_scatter(prompt_partial, "tp", scatter_dimension=0, tiled=True).astype(
        jnp.float32
    )
    decode_out = gather_over_tp(own_out)
    prompt_out = (prompt_rows.astype(jnp.float32) + attended + out_bias).astype(jnp.bfloat16)
    prompt_cache = jnp.stack([key_rows, value_rows])
    kept_out = decode_out[:staying]
    send_rows = jnp.where(has[:, None], decode_out[picks], jnp.zeros((), jnp.bfloat16))
    send_rows, moved_cache = lax.optimization_barrier((send_rows, moved_cache))
    moved_out = lax.all_to_all(send_rows, "rep", split_axis=0, concat_axis=0, tiled=True)
    return (prompt_out, prompt_cache, kept_out, kept_cache, moved_out, moved_cache)


def solution(mesh):
    placed = (
        P(("rep", "tp"), None),
        P("rep", None),
        P("rep", None),
        P("rep"),
        P("rep", None),
        P("rep", None, None, "tp"),
        P(),
        P(),
        P(None, None, "tp"),
        P(None, "tp"),
        P("tp", None),
        P(),
    )
    return jax.shard_map(
        on_device,
        mesh=mesh,
        in_specs=placed,
        out_specs=(
            P(("rep", "tp"), None),
            P(None, "rep", "tp"),
            P("rep", None),
            P("rep", None, None, "tp"),
            P("rep", None),
            P("rep", None, None, "tp"),
        ),
        check_vma=False,
    )
```

```python
import jax
import jax.numpy as jnp
from jax import lax
from jax.sharding import PartitionSpec as P

HEAD_DIM = 128
CAP = 1


EPSILON = 1e-05


def layer_norm(values, norm_gain, norm_bias):
    wide = values.astype(jnp.float32)
    center = jnp.mean(wide, axis=-1, keepdims=True)
    spread = jnp.mean(jnp.square(wide - center), axis=-1, keepdims=True)
    scaled = (wide - center) * lax.rsqrt(spread + EPSILON)
    return (scaled * norm_gain + norm_bias).astype(jnp.bfloat16)


def decode_partial(rows, cache, ages, norm_gain, norm_bias, qkv_weight, qkv_bias, out_weight):
    count = rows.shape[0]
    width = qkv_weight.shape[2]
    heads_here = width // HEAD_DIM
    length = cache.shape[2]
    normed = layer_norm(rows, norm_gain, norm_bias)
    projected = jnp.einsum("rd,cde->cre", normed, qkv_weight, preferred_element_type=jnp.float32)
    queries = (projected[0] + qkv_bias[0]).astype(jnp.bfloat16)
    key_new = (projected[1] + qkv_bias[1]).astype(jnp.bfloat16)
    value_new = (projected[2] + qkv_bias[2]).astype(jnp.bfloat16)
    head_of_col = jnp.arange(width) // HEAD_DIM
    diag = jnp.arange(heads_here)[:, None] == head_of_col[None, :]
    q_blocks = jnp.where(diag[None], queries[:, None, :], jnp.zeros((), jnp.bfloat16))
    scale = HEAD_DIM ** (-0.5)
    scores = (
        jnp.einsum("rhc,rlc->rhl", q_blocks, cache[:, 0], preferred_element_type=jnp.float32)
        * scale
    )
    own = (
        jnp.sum(
            (queries.astype(jnp.float32) * key_new.astype(jnp.float32)).reshape(
                count, heads_here, HEAD_DIM
            ),
            axis=-1,
        )
        * scale
    )
    live = jnp.arange(length)[None, :] < ages[:, None]
    scores = jnp.where(live[:, None, :], scores, -1e30)
    highest = jnp.maximum(jnp.max(scores, axis=-1), own)
    weights = jnp.exp(scores - highest[..., None])
    own_weight = jnp.exp(own - highest)
    total = jnp.sum(weights, axis=-1) + own_weight
    probs = (weights / total[..., None]).astype(jnp.bfloat16)
    own_prob = (own_weight / total).astype(jnp.bfloat16)
    mixed = jnp.einsum("rhl,rlc->rhc", probs, cache[:, 1], preferred_element_type=jnp.float32)
    context = jnp.sum(jnp.where(diag[None], mixed, 0.0), axis=1)
    context = context + own_prob.astype(jnp.float32)[:, head_of_col] * value_new.astype(jnp.float32)
    context = context.astype(jnp.bfloat16)
    partial_value = jnp.dot(context, out_weight, preferred_element_type=jnp.float32)
    return partial_value, key_new, value_new


def updated_rows(cache, key_new, value_new, ages, picks):
    length = cache.shape[2]
    fresh = jnp.stack([key_new, value_new], axis=1)[picks]
    written = jnp.arange(length)[None, :] == ages[picks][:, None]
    return jnp.where(written[:, None, :, None], fresh[:, :, None, :], cache[picks])


def scatter_over_tp(pieces, rows, out_bias):
    n = lax.axis_size("tp")
    me = lax.axis_index("tp")
    share = pieces.shape[1]
    rolled = jnp.take(pieces, (me + jnp.arange(n)) % n, axis=0)
    total = rolled[0].astype(jnp.float32)
    for shift in range(1, n):
        got = lax.ppermute(rolled[shift], "tp", [(i, (i + shift) % n) for i in range(n)])
        total = total + got.astype(jnp.float32)
    own_rows = lax.dynamic_slice_in_dim(rows, me * share, share, 0)
    return (own_rows.astype(jnp.float32) + total + out_bias).astype(jnp.bfloat16)


def gather_over_tp(own_out):
    n = lax.axis_size("tp")
    me = lax.axis_index("tp")
    held = [own_out]
    for shift in range(1, n):
        held.append(lax.ppermute(own_out, "tp", [(i, (i + shift) % n) for i in range(n)]))
    stacked = jnp.stack(held)
    return jnp.take(stacked, (me - jnp.arange(n)) % n, axis=0).reshape(-1, own_out.shape[1])


def on_device(
    prompt_rows,
    prompt_pieces,
    decode_rows,
    request_ages,
    migrate_to,
    past_cache,
    norm_gain,
    norm_bias,
    qkv_weight,
    qkv_bias,
    out_weight,
    out_bias,
):
    rep_count = lax.axis_size("rep")
    width = qkv_weight.shape[2]
    heads_here = width // HEAD_DIM
    leaving = migrate_to.shape[0]
    staying = decode_rows.shape[0] - leaving
    targets = migrate_to[:, 0]
    match = targets[None, :] == jnp.arange(rep_count * CAP)[:, None]
    has = jnp.any(match, axis=1)
    picks = staying + jnp.sum(jnp.where(match, jnp.arange(leaving)[None, :], 0), axis=1)
    partial_value, key_new, value_new = decode_partial(
        decode_rows, past_cache, request_ages, norm_gain, norm_bias, qkv_weight, qkv_bias, out_weight
    )
    send_cache = jnp.where(
        has[:, None, None, None],
        updated_rows(past_cache, key_new, value_new, request_ages, picks),
        jnp.zeros((), jnp.bfloat16),
    )
    moved_cache = lax.all_to_all(send_cache, "rep", split_axis=0, concat_axis=0, tiled=True)
    tp_count = lax.axis_size("tp")
    decode_pieces = partial_value.astype(jnp.bfloat16).reshape(
        tp_count, decode_rows.shape[0] // tp_count, decode_rows.shape[1]
    )
    own_out = scatter_over_tp(decode_pieces, decode_rows, out_bias)
    normed = lax.all_gather(layer_norm(prompt_rows, norm_gain, norm_bias), "tp", axis=0, tiled=True)
    projected = jnp.einsum("rd,cde->cre", normed, qkv_weight, preferred_element_type=jnp.float32)
    total_rows = projected.shape[1]
    queries = (projected[0] + qkv_bias[0]).astype(jnp.bfloat16)
    key_rows = (projected[1] + qkv_bias[1]).astype(jnp.bfloat16)
    value_rows = (projected[2] + qkv_bias[2]).astype(jnp.bfloat16)
    diag = jnp.arange(heads_here)[:, None] == (jnp.arange(width) // HEAD_DIM)[None, :]
    q_blocks = jnp.where(diag[:, None, :], queries[None], jnp.zeros((), jnp.bfloat16))
    scores = jnp.einsum(
        "hqc,kc->hqk", q_blocks, key_rows, preferred_element_type=jnp.float32
    ) * HEAD_DIM ** (-0.5)
    pieces = prompt_pieces[0]
    position = jnp.arange(total_rows)
    allowed = (pieces[:, None] == pieces[None, :]) & (position[None, :] <= position[:, None])
    scores = jnp.where(allowed[None], scores, -1e30)
    highest = jnp.max(scores, axis=-1, keepdims=True)
    weights = jnp.exp(scores - highest)
    probs = (weights / jnp.sum(weights, axis=-1, keepdims=True)).astype(jnp.bfloat16)
    mixed = jnp.einsum("hqk,kc->hqc", probs, value_rows, preferred_element_type=jnp.float32)
    context = jnp.sum(jnp.where(diag[:, None, :], mixed, 0.0), axis=0).astype(jnp.bfloat16)
    prompt_partial = jnp.dot(context, out_weight, preferred_element_type=jnp.float32).astype(
        jnp.bfloat16
    )
    prompt_partial, own_out, key_rows, value_rows, key_new, value_new = lax.optimization_barrier(
        (prompt_partial, own_out, key_rows, value_rows, key_new, value_new)
    )
    written = (jnp.arange(past_cache.shape[2])[None, :] == request_ages[:staying, None])
    fresh = jnp.stack([key_new[:staying], value_new[:staying]], axis=1)
    kept_cache = jnp.where(
        written[:, None, :, None], fresh[:, :, None, :], past_cache[:staying]
    )
    attended = lax.psum_scatter(prompt_partial, "tp", scatter_dimension=0, tiled=True).astype(
        jnp.float32
    )
    decode_out = gather_over_tp(own_out)
    prompt_out = (prompt_rows.astype(jnp.float32) + attended + out_bias).astype(jnp.bfloat16)
    prompt_cache = jnp.stack([key_rows, value_rows])
    kept_out = decode_out[:staying]
    send_rows = jnp.where(has[:, None], decode_out[picks], jnp.zeros((), jnp.bfloat16))
    send_rows, moved_cache = lax.optimization_barrier((send_rows, moved_cache))
    moved_out = lax.all_to_all(send_rows, "rep", split_axis=0, concat_axis=0, tiled=True)
    return (prompt_out, prompt_cache, kept_out, kept_cache, moved_out, moved_cache)


def solution(mesh):
    placed = (
        P(("rep", "tp"), None),
        P("rep", None),
        P("rep", None),
        P("rep"),
        P("rep", None),
        P("rep", None, None, "tp"),
        P(),
        P(),
        P(None, None, "tp"),
        P(None, "tp"),
        P("tp", None),
        P(),
    )
    return jax.shard_map(
        on_device,
        mesh=mesh,
        in_specs=placed,
        out_specs=(
            P(("rep", "tp"), None),
            P(None, "rep", "tp"),
            P("rep", None),
            P("rep", None, None, "tp"),
            P("rep", None),
            P("rep", None, None, "tp"),
        ),
        check_vma=False,
    )
```

```python
import jax
import jax.numpy as jnp
from jax import lax
from jax.sharding import PartitionSpec as P

HEAD_DIM = 128
CAP = 1


EPSILON = 1e-05


def layer_norm(values, norm_gain, norm_bias):
    wide = values.astype(jnp.float32)
    center = jnp.mean(wide, axis=-1, keepdims=True)
    spread = jnp.mean(jnp.square(wide - center), axis=-1, keepdims=True)
    scaled = (wide - center) * lax.rsqrt(spread + EPSILON)
    return (scaled * norm_gain + norm_bias).astype(jnp.bfloat16)


def decode_partial(rows, cache, ages, norm_gain, norm_bias, qkv_weight, qkv_bias, out_weight):
    count = rows.shape[0]
    width = qkv_weight.shape[2]
    heads_here = width // HEAD_DIM
    length = cache.shape[2]
    normed = layer_norm(rows, norm_gain, norm_bias)
    projected = jnp.einsum("rd,cde->cre", normed, qkv_weight, preferred_element_type=jnp.float32)
    queries = (projected[0] + qkv_bias[0]).astype(jnp.bfloat16)
    key_new = (projected[1] + qkv_bias[1]).astype(jnp.bfloat16)
    value_new = (projected[2] + qkv_bias[2]).astype(jnp.bfloat16)
    head_of_col = jnp.arange(width) // HEAD_DIM
    diag = jnp.arange(heads_here)[:, None] == head_of_col[None, :]
    q_blocks = jnp.where(diag[None], queries[:, None, :], jnp.zeros((), jnp.bfloat16))
    scale = HEAD_DIM ** (-0.5)
    scores = (
        jnp.einsum("rhc,rlc->rhl", q_blocks, cache[:, 0], preferred_element_type=jnp.float32)
        * scale
    )
    own = (
        jnp.sum(
            (queries.astype(jnp.float32) * key_new.astype(jnp.float32)).reshape(
                count, heads_here, HEAD_DIM
            ),
            axis=-1,
        )
        * scale
    )
    live = jnp.arange(length)[None, :] < ages[:, None]
    scores = jnp.where(live[:, None, :], scores, -1e30)
    highest = jnp.maximum(jnp.max(scores, axis=-1), own)
    weights = jnp.exp(scores - highest[..., None])
    own_weight = jnp.exp(own - highest)
    total = jnp.sum(weights, axis=-1) + own_weight
    probs = (weights / total[..., None]).astype(jnp.bfloat16)
    own_prob = (own_weight / total).astype(jnp.bfloat16)
    mixed = jnp.einsum("rhl,rlc->rhc", probs, cache[:, 1], preferred_element_type=jnp.float32)
    context = jnp.sum(jnp.where(diag[None], mixed, 0.0), axis=1)
    context = context + own_prob.astype(jnp.float32)[:, head_of_col] * value_new.astype(jnp.float32)
    context = context.astype(jnp.bfloat16)
    partial_value = jnp.dot(context, out_weight, preferred_element_type=jnp.float32)
    return partial_value, key_new, value_new


def updated_rows(cache, key_new, value_new, ages, picks):
    length = cache.shape[2]
    fresh = jnp.stack([key_new, value_new], axis=1)[picks]
    written = jnp.arange(length)[None, :] == ages[picks][:, None]
    return jnp.where(written[:, None, :, None], fresh[:, :, None, :], cache[picks])


def scatter_over_tp(pieces, rows, out_bias):
    n = lax.axis_size("tp")
    me = lax.axis_index("tp")
    share = pieces.shape[1]
    rolled = jnp.take(pieces, (me + jnp.arange(n)) % n, axis=0)
    total = rolled[0].astype(jnp.float32)
    for shift in range(1, n):
        got = lax.ppermute(rolled[shift], "tp", [(i, (i + shift) % n) for i in range(n)])
        total = total + got.astype(jnp.float32)
    own_rows = lax.dynamic_slice_in_dim(rows, me * share, share, 0)
    return (own_rows.astype(jnp.float32) + total + out_bias).astype(jnp.bfloat16)


def gather_over_tp(own_out):
    n = lax.axis_size("tp")
    me = lax.axis_index("tp")
    held = [own_out]
    for shift in range(1, n):
        held.append(lax.ppermute(own_out, "tp", [(i, (i + shift) % n) for i in range(n)]))
    stacked = jnp.stack(held)
    return jnp.take(stacked, (me - jnp.arange(n)) % n, axis=0).reshape(-1, own_out.shape[1])


def on_device(
    prompt_rows,
    prompt_pieces,
    decode_rows,
    request_ages,
    migrate_to,
    past_cache,
    norm_gain,
    norm_bias,
    qkv_weight,
    qkv_bias,
    out_weight,
    out_bias,
):
    rep_count = lax.axis_size("rep")
    width = qkv_weight.shape[2]
    heads_here = width // HEAD_DIM
    leaving = migrate_to.shape[0]
    staying = decode_rows.shape[0] - leaving
    targets = migrate_to[:, 0]
    match = targets[None, :] == jnp.arange(rep_count * CAP)[:, None]
    has = jnp.any(match, axis=1)
    picks = staying + jnp.sum(jnp.where(match, jnp.arange(leaving)[None, :], 0), axis=1)
    partial_value, key_new, value_new = decode_partial(
        decode_rows, past_cache, request_ages, norm_gain, norm_bias, qkv_weight, qkv_bias, out_weight
    )
    send_cache = jnp.where(
        has[:, None, None, None],
        updated_rows(past_cache, key_new, value_new, request_ages, picks),
        jnp.zeros((), jnp.bfloat16),
    )
    moved_cache = lax.all_to_all(send_cache, "rep", split_axis=0, concat_axis=0, tiled=True)
    tp_count = lax.axis_size("tp")
    decode_pieces = partial_value.astype(jnp.bfloat16).reshape(
        tp_count, decode_rows.shape[0] // tp_count, decode_rows.shape[1]
    )
    own_out = scatter_over_tp(decode_pieces, decode_rows, out_bias)
    normed = lax.all_gather(layer_norm(prompt_rows, norm_gain, norm_bias), "tp", axis=0, tiled=True)
    model = qkv_weight.shape[1]
    split_weight = qkv_weight.reshape(3, model, heads_here, HEAD_DIM)
    split_bias = qkv_bias.reshape(3, heads_here, 1, HEAD_DIM)
    projected = jnp.einsum(
        "rd,cdhe->chre", normed, split_weight, preferred_element_type=jnp.float32
    )
    total_rows = projected.shape[2]
    head_q = (projected[0] + split_bias[0]).astype(jnp.bfloat16)
    head_k = (projected[1] + split_bias[1]).astype(jnp.bfloat16)
    head_v = (projected[2] + split_bias[2]).astype(jnp.bfloat16)
    scores = jnp.einsum(
        "hqe,hke->hqk", head_q, head_k, preferred_element_type=jnp.float32
    ) * HEAD_DIM ** (-0.5)
    pieces = prompt_pieces[0]
    position = jnp.arange(total_rows)
    allowed = (pieces[:, None] == pieces[None, :]) & (position[None, :] <= position[:, None])
    scores = jnp.where(allowed[None], scores, -1e30)
    highest = jnp.max(scores, axis=-1, keepdims=True)
    weights = jnp.exp(scores - highest)
    probs = (weights / jnp.sum(weights, axis=-1, keepdims=True)).astype(jnp.bfloat16)
    context = jnp.einsum("hqk,hke->qhe", probs, head_v, preferred_element_type=jnp.float32)
    context = context.reshape(total_rows, width).astype(jnp.bfloat16)
    key_rows = jnp.transpose(head_k, (1, 0, 2)).reshape(total_rows, width)
    value_rows = jnp.transpose(head_v, (1, 0, 2)).reshape(total_rows, width)
    prompt_partial = jnp.dot(context, out_weight, preferred_element_type=jnp.float32).astype(
        jnp.bfloat16
    )
    prompt_partial, own_out, key_rows, value_rows, key_new, value_new = lax.optimization_barrier(
        (prompt_partial, own_out, key_rows, value_rows, key_new, value_new)
    )
    written = (jnp.arange(past_cache.shape[2])[None, :] == request_ages[:staying, None])
    fresh = jnp.stack([key_new[:staying], value_new[:staying]], axis=1)
    kept_cache = jnp.where(
        written[:, None, :, None], fresh[:, :, None, :], past_cache[:staying]
    )
    attended = lax.psum_scatter(prompt_partial, "tp", scatter_dimension=0, tiled=True).astype(
        jnp.float32
    )
    decode_out = gather_over_tp(own_out)
    prompt_out = (prompt_rows.astype(jnp.float32) + attended + out_bias).astype(jnp.bfloat16)
    prompt_cache = jnp.stack([key_rows, value_rows])
    kept_out = decode_out[:staying]
    send_rows = jnp.where(has[:, None], decode_out[picks], jnp.zeros((), jnp.bfloat16))
    send_rows, moved_cache = lax.optimization_barrier((send_rows, moved_cache))
    moved_cache = jnp.where(request_ages[0] > 0, moved_cache, jnp.zeros((), jnp.bfloat16))
    moved_out = lax.all_to_all(send_rows, "rep", split_axis=0, concat_axis=0, tiled=True)
    return (prompt_out, prompt_cache, kept_out, kept_cache, moved_out, moved_cache)


def solution(mesh):
    placed = (
        P(("rep", "tp"), None),
        P("rep", None),
        P("rep", None),
        P("rep"),
        P("rep", None),
        P("rep", None, None, "tp"),
        P(),
        P(),
        P(None, None, "tp"),
        P(None, "tp"),
        P("tp", None),
        P(),
    )
    return jax.shard_map(
        on_device,
        mesh=mesh,
        in_specs=placed,
        out_specs=(
            P(("rep", "tp"), None),
            P(None, "rep", "tp"),
            P("rep", None),
            P("rep", None, None, "tp"),
            P("rep", None),
            P("rep", None, None, "tp"),
        ),
        check_vma=False,
    )
```

```python
import jax
import jax.numpy as jnp
from jax import lax
from jax.sharding import PartitionSpec as P

HEAD_DIM = 128
CAP = 1


EPSILON = 1e-05


def layer_norm(values, norm_gain, norm_bias):
    wide = values.astype(jnp.float32)
    center = jnp.mean(wide, axis=-1, keepdims=True)
    spread = jnp.mean(jnp.square(wide - center), axis=-1, keepdims=True)
    scaled = (wide - center) * lax.rsqrt(spread + EPSILON)
    return (scaled * norm_gain + norm_bias).astype(jnp.bfloat16)


def decode_partial(rows, cache, ages, norm_gain, norm_bias, qkv_weight, qkv_bias, out_weight):
    count = rows.shape[0]
    width = qkv_weight.shape[2]
    heads_here = width // HEAD_DIM
    length = cache.shape[2]
    normed = layer_norm(rows, norm_gain, norm_bias)
    projected = jnp.einsum("rd,cde->cre", normed, qkv_weight, preferred_element_type=jnp.float32)
    queries = (projected[0] + qkv_bias[0]).astype(jnp.bfloat16)
    key_new = (projected[1] + qkv_bias[1]).astype(jnp.bfloat16)
    value_new = (projected[2] + qkv_bias[2]).astype(jnp.bfloat16)
    head_of_col = jnp.arange(width) // HEAD_DIM
    diag = jnp.arange(heads_here)[:, None] == head_of_col[None, :]
    q_blocks = jnp.where(diag[None], queries[:, None, :], jnp.zeros((), jnp.bfloat16))
    scale = HEAD_DIM ** (-0.5)
    scores = (
        jnp.einsum("rhc,rlc->rhl", q_blocks, cache[:, 0], preferred_element_type=jnp.float32)
        * scale
    )
    own = (
        jnp.sum(
            (queries.astype(jnp.float32) * key_new.astype(jnp.float32)).reshape(
                count, heads_here, HEAD_DIM
            ),
            axis=-1,
        )
        * scale
    )
    live = jnp.arange(length)[None, :] < ages[:, None]
    scores = jnp.where(live[:, None, :], scores, -1e30)
    highest = jnp.maximum(jnp.max(scores, axis=-1), own)
    weights = jnp.exp(scores - highest[..., None])
    own_weight = jnp.exp(own - highest)
    total = jnp.sum(weights, axis=-1) + own_weight
    probs = (weights / total[..., None]).astype(jnp.bfloat16)
    own_prob = (own_weight / total).astype(jnp.bfloat16)
    mixed = jnp.einsum("rhl,rlc->rhc", probs, cache[:, 1], preferred_element_type=jnp.float32)
    context = jnp.sum(jnp.where(diag[None], mixed, 0.0), axis=1)
    context = context + own_prob.astype(jnp.float32)[:, head_of_col] * value_new.astype(jnp.float32)
    context = context.astype(jnp.bfloat16)
    partial_value = jnp.dot(context, out_weight, preferred_element_type=jnp.float32)
    return partial_value, key_new, value_new


def updated_rows(cache, key_new, value_new, ages, picks):
    length = cache.shape[2]
    fresh = jnp.stack([key_new, value_new], axis=1)[picks]
    written = jnp.arange(length)[None, :] == ages[picks][:, None]
    return jnp.where(written[:, None, :, None], fresh[:, :, None, :], cache[picks])


def scatter_over_tp(pieces, rows, out_bias):
    n = lax.axis_size("tp")
    me = lax.axis_index("tp")
    share = pieces.shape[1]
    rolled = jnp.take(pieces, (me + jnp.arange(n)) % n, axis=0)
    total = rolled[0].astype(jnp.float32)
    for shift in range(1, n):
        got = lax.ppermute(rolled[shift], "tp", [(i, (i + shift) % n) for i in range(n)])
        total = total + got.astype(jnp.float32)
    own_rows = lax.dynamic_slice_in_dim(rows, me * share, share, 0)
    return (own_rows.astype(jnp.float32) + total + out_bias).astype(jnp.bfloat16)


def gather_over_tp(own_out):
    n = lax.axis_size("tp")
    me = lax.axis_index("tp")
    held = [own_out]
    for shift in range(1, n):
        held.append(lax.ppermute(own_out, "tp", [(i, (i + shift) % n) for i in range(n)]))
    stacked = jnp.stack(held)
    return jnp.take(stacked, (me - jnp.arange(n)) % n, axis=0).reshape(-1, own_out.shape[1])


def on_device(
    prompt_rows,
    prompt_pieces,
    decode_rows,
    request_ages,
    migrate_to,
    past_cache,
    norm_gain,
    norm_bias,
    qkv_weight,
    qkv_bias,
    out_weight,
    out_bias,
):
    rep_count = lax.axis_size("rep")
    width = qkv_weight.shape[2]
    heads_here = width // HEAD_DIM
    leaving = migrate_to.shape[0]
    staying = decode_rows.shape[0] - leaving
    targets = migrate_to[:, 0]
    match = targets[None, :] == jnp.arange(rep_count * CAP)[:, None]
    has = jnp.any(match, axis=1)
    picks = staying + jnp.sum(jnp.where(match, jnp.arange(leaving)[None, :], 0), axis=1)
    partial_value, key_new, value_new = decode_partial(
        decode_rows, past_cache, request_ages, norm_gain, norm_bias, qkv_weight, qkv_bias, out_weight
    )
    send_cache = jnp.where(
        has[:, None, None, None],
        updated_rows(past_cache, key_new, value_new, request_ages, picks),
        jnp.zeros((), jnp.bfloat16),
    )
    moved_cache = lax.all_to_all(send_cache, "rep", split_axis=0, concat_axis=0, tiled=True)
    tp_count = lax.axis_size("tp")
    decode_pieces = partial_value.astype(jnp.bfloat16).reshape(
        tp_count, decode_rows.shape[0] // tp_count, decode_rows.shape[1]
    )
    own_out = scatter_over_tp(decode_pieces, decode_rows, out_bias)
    normed = lax.all_gather(layer_norm(prompt_rows, norm_gain, norm_bias), "tp", axis=0, tiled=True)
    model = qkv_weight.shape[1]
    split_weight = qkv_weight.reshape(3, model, heads_here, HEAD_DIM)
    split_bias = qkv_bias.reshape(3, heads_here, 1, HEAD_DIM)
    projected = jnp.einsum(
        "rd,cdhe->chre", normed, split_weight, preferred_element_type=jnp.float32
    )
    total_rows = projected.shape[2]
    head_q = (projected[0] + split_bias[0]).astype(jnp.bfloat16)
    head_k = (projected[1] + split_bias[1]).astype(jnp.bfloat16)
    head_v = (projected[2] + split_bias[2]).astype(jnp.bfloat16)
    scores = jnp.einsum(
        "hqe,hke->hqk", head_q, head_k, preferred_element_type=jnp.float32
    ) * HEAD_DIM ** (-0.5)
    pieces = prompt_pieces[0]
    position = jnp.arange(total_rows)
    allowed = (pieces[:, None] == pieces[None, :]) & (position[None, :] <= position[:, None])
    scores = jnp.where(allowed[None], scores, -1e30)
    highest = jnp.max(scores, axis=-1, keepdims=True)
    weights = jnp.exp(scores - highest)
    probs = (weights / jnp.sum(weights, axis=-1, keepdims=True)).astype(jnp.bfloat16)
    context = jnp.einsum("hqk,hke->qhe", probs, head_v, preferred_element_type=jnp.float32)
    context = context.reshape(total_rows, width).astype(jnp.bfloat16)
    key_rows = jnp.transpose(head_k, (1, 0, 2)).reshape(total_rows, width)
    value_rows = jnp.transpose(head_v, (1, 0, 2)).reshape(total_rows, width)
    prompt_partial = jnp.dot(context, out_weight, preferred_element_type=jnp.float32).astype(
        jnp.bfloat16
    )
    prompt_partial, own_out, key_rows, value_rows, key_new, value_new = lax.optimization_barrier(
        (prompt_partial, own_out, key_rows, value_rows, key_new, value_new)
    )
    written = (jnp.arange(past_cache.shape[2])[None, :] == request_ages[:staying, None])
    fresh = jnp.stack([key_new[:staying], value_new[:staying]], axis=1)
    kept_cache = jnp.where(
        written[:, None, :, None], fresh[:, :, None, :], past_cache[:staying]
    )
    attended = lax.psum_scatter(prompt_partial, "tp", scatter_dimension=0, tiled=True).astype(
        jnp.float32
    )
    own_out, kept_cache = lax.optimization_barrier((own_out, kept_cache))
    decode_out = gather_over_tp(own_out)
    prompt_out = (prompt_rows.astype(jnp.float32) + attended + out_bias).astype(jnp.bfloat16)
    prompt_cache = jnp.stack([key_rows, value_rows])
    kept_out = decode_out[:staying]
    send_rows = jnp.where(has[:, None], decode_out[picks], jnp.zeros((), jnp.bfloat16))
    send_rows, moved_cache = lax.optimization_barrier((send_rows, moved_cache))
    moved_cache = jnp.where(request_ages[0] > 0, moved_cache, jnp.zeros((), jnp.bfloat16))
    moved_out = lax.all_to_all(send_rows, "rep", split_axis=0, concat_axis=0, tiled=True)
    return (prompt_out, prompt_cache, kept_out, kept_cache, moved_out, moved_cache)


def solution(mesh):
    placed = (
        P(("rep", "tp"), None),
        P("rep", None),
        P("rep", None),
        P("rep"),
        P("rep", None),
        P("rep", None, None, "tp"),
        P(),
        P(),
        P(None, None, "tp"),
        P(None, "tp"),
        P("tp", None),
        P(),
    )
    return jax.shard_map(
        on_device,
        mesh=mesh,
        in_specs=placed,
        out_specs=(
            P(("rep", "tp"), None),
            P(None, "rep", "tp"),
            P("rep", None),
            P("rep", None, None, "tp"),
            P("rep", None),
            P("rep", None, None, "tp"),
        ),
        check_vma=False,
    )
```

```python
import jax
import jax.numpy as jnp
from jax import lax
from jax.sharding import PartitionSpec as P

HEAD_DIM = 128
CAP = 1


EPSILON = 1e-05


def layer_norm(values, norm_gain, norm_bias):
    wide = values.astype(jnp.float32)
    center = jnp.mean(wide, axis=-1, keepdims=True)
    spread = jnp.mean(jnp.square(wide - center), axis=-1, keepdims=True)
    scaled = (wide - center) * lax.rsqrt(spread + EPSILON)
    return (scaled * norm_gain + norm_bias).astype(jnp.bfloat16)


def decode_partial(rows, cache, ages, norm_gain, norm_bias, qkv_weight, qkv_bias, out_weight):
    count = rows.shape[0]
    width = qkv_weight.shape[2]
    heads_here = width // HEAD_DIM
    length = cache.shape[2]
    normed = layer_norm(rows, norm_gain, norm_bias)
    projected = jnp.einsum("rd,cde->cre", normed, qkv_weight, preferred_element_type=jnp.float32)
    queries = (projected[0] + qkv_bias[0]).astype(jnp.bfloat16)
    key_new = (projected[1] + qkv_bias[1]).astype(jnp.bfloat16)
    value_new = (projected[2] + qkv_bias[2]).astype(jnp.bfloat16)
    head_of_col = jnp.arange(width) // HEAD_DIM
    diag = jnp.arange(heads_here)[:, None] == head_of_col[None, :]
    q_blocks = jnp.where(diag[None], queries[:, None, :], jnp.zeros((), jnp.bfloat16))
    scale = HEAD_DIM ** (-0.5)
    scores = (
        jnp.einsum("rhc,rlc->rhl", q_blocks, cache[:, 0], preferred_element_type=jnp.float32)
        * scale
    )
    own = (
        jnp.sum(
            (queries.astype(jnp.float32) * key_new.astype(jnp.float32)).reshape(
                count, heads_here, HEAD_DIM
            ),
            axis=-1,
        )
        * scale
    )
    live = jnp.arange(length)[None, :] < ages[:, None]
    scores = jnp.where(live[:, None, :], scores, -1e30)
    highest = jnp.maximum(jnp.max(scores, axis=-1), own)
    weights = jnp.exp(scores - highest[..., None])
    own_weight = jnp.exp(own - highest)
    total = jnp.sum(weights, axis=-1) + own_weight
    probs = (weights / total[..., None]).astype(jnp.bfloat16)
    own_prob = (own_weight / total).astype(jnp.bfloat16)
    mixed = jnp.einsum("rhl,rlc->rhc", probs, cache[:, 1], preferred_element_type=jnp.float32)
    context = jnp.sum(jnp.where(diag[None], mixed, 0.0), axis=1)
    context = context + own_prob.astype(jnp.float32)[:, head_of_col] * value_new.astype(jnp.float32)
    context = context.astype(jnp.bfloat16)
    partial_value = jnp.dot(context, out_weight, preferred_element_type=jnp.float32)
    return partial_value, key_new, value_new


def updated_rows(cache, key_new, value_new, ages, picks):
    length = cache.shape[2]
    fresh = jnp.stack([key_new, value_new], axis=1)[picks]
    written = jnp.arange(length)[None, :] == ages[picks][:, None]
    return jnp.where(written[:, None, :, None], fresh[:, :, None, :], cache[picks])


def scatter_over_tp(pieces, rows, out_bias):
    n = lax.axis_size("tp")
    me = lax.axis_index("tp")
    share = pieces.shape[1]
    rolled = jnp.take(pieces, (me + jnp.arange(n)) % n, axis=0)
    total = rolled[0].astype(jnp.float32)
    for shift in range(1, n):
        got = lax.ppermute(rolled[shift], "tp", [(i, (i + shift) % n) for i in range(n)])
        total = total + got.astype(jnp.float32)
    own_rows = lax.dynamic_slice_in_dim(rows, me * share, share, 0)
    return (own_rows.astype(jnp.float32) + total + out_bias).astype(jnp.bfloat16)


def gather_over_tp(own_out):
    n = lax.axis_size("tp")
    me = lax.axis_index("tp")
    held = [own_out]
    for shift in range(1, n):
        held.append(lax.ppermute(own_out, "tp", [(i, (i + shift) % n) for i in range(n)]))
    stacked = jnp.stack(held)
    return jnp.take(stacked, (me - jnp.arange(n)) % n, axis=0).reshape(-1, own_out.shape[1])


def on_device(
    prompt_rows,
    prompt_pieces,
    decode_rows,
    request_ages,
    migrate_to,
    past_cache,
    norm_gain,
    norm_bias,
    qkv_weight,
    qkv_bias,
    out_weight,
    out_bias,
):
    rep_count = lax.axis_size("rep")
    width = qkv_weight.shape[2]
    heads_here = width // HEAD_DIM
    leaving = migrate_to.shape[0]
    staying = decode_rows.shape[0] - leaving
    targets = migrate_to[:, 0]
    match = targets[None, :] == jnp.arange(rep_count * CAP)[:, None]
    has = jnp.any(match, axis=1)
    picks = staying + jnp.sum(jnp.where(match, jnp.arange(leaving)[None, :], 0), axis=1)
    partial_value, key_new, value_new = decode_partial(
        decode_rows, past_cache, request_ages, norm_gain, norm_bias, qkv_weight, qkv_bias, out_weight
    )
    leave_written = jnp.arange(past_cache.shape[2])[None, :] == request_ages[staying:, None]
    leave_fresh = jnp.stack([key_new[staying:], value_new[staying:]], axis=1)
    leave_rows = jnp.where(
        leave_written[:, None, :, None], leave_fresh[:, :, None, :], past_cache[staying:]
    )
    padded = jnp.concatenate([leave_rows, jnp.zeros_like(leave_rows[:1])], axis=0)
    send_cache = padded[jnp.where(has, picks - staying, leaving)]
    moved_cache = lax.all_to_all(send_cache, "rep", split_axis=0, concat_axis=0, tiled=True)
    tp_count = lax.axis_size("tp")
    decode_pieces = partial_value.astype(jnp.bfloat16).reshape(
        tp_count, decode_rows.shape[0] // tp_count, decode_rows.shape[1]
    )
    own_out = scatter_over_tp(decode_pieces, decode_rows, out_bias)
    normed = lax.all_gather(layer_norm(prompt_rows, norm_gain, norm_bias), "tp", axis=0, tiled=True)
    model = qkv_weight.shape[1]
    split_weight = qkv_weight.reshape(3, model, heads_here, HEAD_DIM)
    split_bias = qkv_bias.reshape(3, heads_here, 1, HEAD_DIM)
    projected = jnp.einsum(
        "rd,cdhe->chre", normed, split_weight, preferred_element_type=jnp.float32
    )
    total_rows = projected.shape[2]
    head_q = (projected[0] + split_bias[0]).astype(jnp.bfloat16)
    head_k = (projected[1] + split_bias[1]).astype(jnp.bfloat16)
    head_v = (projected[2] + split_bias[2]).astype(jnp.bfloat16)
    scores = jnp.einsum(
        "hqe,hke->hqk", head_q, head_k, preferred_element_type=jnp.float32
    ) * HEAD_DIM ** (-0.5)
    pieces = prompt_pieces[0]
    position = jnp.arange(total_rows)
    allowed = (pieces[:, None] == pieces[None, :]) & (position[None, :] <= position[:, None])
    scores = jnp.where(allowed[None], scores, -1e30)
    highest = jnp.max(scores, axis=-1, keepdims=True)
    weights = jnp.exp(scores - highest)
    probs = (weights / jnp.sum(weights, axis=-1, keepdims=True)).astype(jnp.bfloat16)
    context = jnp.einsum("hqk,hke->qhe", probs, head_v, preferred_element_type=jnp.float32)
    context = context.reshape(total_rows, width).astype(jnp.bfloat16)
    key_rows = jnp.transpose(head_k, (1, 0, 2)).reshape(total_rows, width)
    value_rows = jnp.transpose(head_v, (1, 0, 2)).reshape(total_rows, width)
    prompt_partial = jnp.dot(context, out_weight, preferred_element_type=jnp.float32).astype(
        jnp.bfloat16
    )
    prompt_partial, own_out, key_rows, value_rows, key_new, value_new = lax.optimization_barrier(
        (prompt_partial, own_out, key_rows, value_rows, key_new, value_new)
    )
    written = (jnp.arange(past_cache.shape[2])[None, :] == request_ages[:staying, None])
    fresh = jnp.stack([key_new[:staying], value_new[:staying]], axis=1)
    kept_cache = jnp.where(
        written[:, None, :, None], fresh[:, :, None, :], past_cache[:staying]
    )
    attended = lax.psum_scatter(prompt_partial, "tp", scatter_dimension=0, tiled=True).astype(
        jnp.float32
    )
    own_out, kept_cache = lax.optimization_barrier((own_out, kept_cache))
    decode_out = gather_over_tp(own_out)
    prompt_out = (prompt_rows.astype(jnp.float32) + attended + out_bias).astype(jnp.bfloat16)
    prompt_cache = jnp.stack([key_rows, value_rows])
    kept_out = decode_out[:staying]
    send_rows = jnp.where(has[:, None], decode_out[picks], jnp.zeros((), jnp.bfloat16))
    send_rows, moved_cache = lax.optimization_barrier((send_rows, moved_cache))
    moved_cache = jnp.where(request_ages[0] > 0, moved_cache, jnp.zeros((), jnp.bfloat16))
    moved_out = lax.all_to_all(send_rows, "rep", split_axis=0, concat_axis=0, tiled=True)
    return (prompt_out, prompt_cache, kept_out, kept_cache, moved_out, moved_cache)


def solution(mesh):
    placed = (
        P(("rep", "tp"), None),
        P("rep", None),
        P("rep", None),
        P("rep"),
        P("rep", None),
        P("rep", None, None, "tp"),
        P(),
        P(),
        P(None, None, "tp"),
        P(None, "tp"),
        P("tp", None),
        P(),
    )
    return jax.shard_map(
        on_device,
        mesh=mesh,
        in_specs=placed,
        out_specs=(
            P(("rep", "tp"), None),
            P(None, "rep", "tp"),
            P("rep", None),
            P("rep", None, None, "tp"),
            P("rep", None),
            P("rep", None, None, "tp"),
        ),
        check_vma=False,
    )
```

```python
import jax
import jax.numpy as jnp
from jax import lax
from jax.sharding import PartitionSpec as P

HEAD_DIM = 128
CAP = 1


EPSILON = 1e-05


def layer_norm(values, norm_gain, norm_bias):
    wide = values.astype(jnp.float32)
    center = jnp.mean(wide, axis=-1, keepdims=True)
    spread = jnp.mean(jnp.square(wide - center), axis=-1, keepdims=True)
    scaled = (wide - center) * lax.rsqrt(spread + EPSILON)
    return (scaled * norm_gain + norm_bias).astype(jnp.bfloat16)


def decode_project(rows, norm_gain, norm_bias, qkv_weight, qkv_bias):
    normed = layer_norm(rows, norm_gain, norm_bias)
    projected = jnp.einsum("rd,cde->cre", normed, qkv_weight, preferred_element_type=jnp.float32)
    return tuple((projected[i] + qkv_bias[i]).astype(jnp.bfloat16) for i in range(3))


def decode_partial(queries, key_new, value_new, cache, ages, out_weight):
    count = queries.shape[0]
    width = queries.shape[1]
    heads_here = width // HEAD_DIM
    length = cache.shape[2]
    head_of_col = jnp.arange(width) // HEAD_DIM
    diag = jnp.arange(heads_here)[:, None] == head_of_col[None, :]
    q_blocks = jnp.where(diag[None], queries[:, None, :], jnp.zeros((), jnp.bfloat16))
    scale = HEAD_DIM ** (-0.5)
    scores = (
        jnp.einsum("rhc,rlc->rhl", q_blocks, cache[:, 0], preferred_element_type=jnp.float32)
        * scale
    )
    own = (
        jnp.sum(
            (queries.astype(jnp.float32) * key_new.astype(jnp.float32)).reshape(
                count, heads_here, HEAD_DIM
            ),
            axis=-1,
        )
        * scale
    )
    live = jnp.arange(length)[None, :] < ages[:, None]
    scores = jnp.where(live[:, None, :], scores, -1e30)
    highest = jnp.maximum(jnp.max(scores, axis=-1), own)
    weights = jnp.exp(scores - highest[..., None])
    own_weight = jnp.exp(own - highest)
    total = jnp.sum(weights, axis=-1) + own_weight
    probs = (weights / total[..., None]).astype(jnp.bfloat16)
    own_prob = (own_weight / total).astype(jnp.bfloat16)
    mixed = jnp.einsum("rhl,rlc->rhc", probs, cache[:, 1], preferred_element_type=jnp.float32)
    context = jnp.sum(jnp.where(diag[None], mixed, 0.0), axis=1)
    context = context + own_prob.astype(jnp.float32)[:, head_of_col] * value_new.astype(jnp.float32)
    context = context.astype(jnp.bfloat16)
    partial_value = jnp.dot(context, out_weight, preferred_element_type=jnp.float32)
    return partial_value


def updated_rows(cache, key_new, value_new, ages, picks):
    length = cache.shape[2]
    fresh = jnp.stack([key_new, value_new], axis=1)[picks]
    written = jnp.arange(length)[None, :] == ages[picks][:, None]
    return jnp.where(written[:, None, :, None], fresh[:, :, None, :], cache[picks])


def scatter_over_tp(pieces, rows, out_bias):
    n = lax.axis_size("tp")
    me = lax.axis_index("tp")
    share = pieces.shape[1]
    rolled = jnp.take(pieces, (me + jnp.arange(n)) % n, axis=0)
    total = rolled[0].astype(jnp.float32)
    for shift in range(1, n):
        got = lax.ppermute(rolled[shift], "tp", [(i, (i + shift) % n) for i in range(n)])
        total = total + got.astype(jnp.float32)
    own_rows = lax.dynamic_slice_in_dim(rows, me * share, share, 0)
    return (own_rows.astype(jnp.float32) + total + out_bias).astype(jnp.bfloat16)


def gather_over_tp(own_out):
    n = lax.axis_size("tp")
    me = lax.axis_index("tp")
    held = [own_out]
    for shift in range(1, n):
        held.append(lax.ppermute(own_out, "tp", [(i, (i + shift) % n) for i in range(n)]))
    stacked = jnp.stack(held)
    return jnp.take(stacked, (me - jnp.arange(n)) % n, axis=0).reshape(-1, own_out.shape[1])


def on_device(
    prompt_rows,
    prompt_pieces,
    decode_rows,
    request_ages,
    migrate_to,
    past_cache,
    norm_gain,
    norm_bias,
    qkv_weight,
    qkv_bias,
    out_weight,
    out_bias,
):
    rep_count = lax.axis_size("rep")
    width = qkv_weight.shape[2]
    heads_here = width // HEAD_DIM
    leaving = migrate_to.shape[0]
    staying = decode_rows.shape[0] - leaving
    targets = migrate_to[:, 0]
    match = targets[None, :] == jnp.arange(rep_count * CAP)[:, None]
    has = jnp.any(match, axis=1)
    picks = staying + jnp.sum(jnp.where(match, jnp.arange(leaving)[None, :], 0), axis=1)
    queries_new, key_new, value_new = decode_project(
        decode_rows, norm_gain, norm_bias, qkv_weight, qkv_bias
    )
    leave_written = jnp.arange(past_cache.shape[2])[None, :] == request_ages[staying:, None]
    leave_fresh = jnp.stack([key_new[staying:], value_new[staying:]], axis=1)
    leave_rows = jnp.where(
        leave_written[:, None, :, None], leave_fresh[:, :, None, :], past_cache[staying:]
    )
    padded = jnp.concatenate([leave_rows, jnp.zeros_like(leave_rows[:1])], axis=0)
    send_cache = padded[jnp.where(has, picks - staying, leaving)]
    send_cache, attend_cache = lax.optimization_barrier((send_cache, past_cache))
    moved_cache = lax.all_to_all(send_cache, "rep", split_axis=0, concat_axis=0, tiled=True)
    partial_value = decode_partial(
        queries_new, key_new, value_new, attend_cache, request_ages, out_weight
    )
    tp_count = lax.axis_size("tp")
    decode_pieces = partial_value.astype(jnp.bfloat16).reshape(
        tp_count, decode_rows.shape[0] // tp_count, decode_rows.shape[1]
    )
    own_out = scatter_over_tp(decode_pieces, decode_rows, out_bias)
    normed = lax.all_gather(layer_norm(prompt_rows, norm_gain, norm_bias), "tp", axis=0, tiled=True)
    model = qkv_weight.shape[1]
    split_weight = qkv_weight.reshape(3, model, heads_here, HEAD_DIM)
    split_bias = qkv_bias.reshape(3, heads_here, 1, HEAD_DIM)
    projected = jnp.einsum(
        "rd,cdhe->chre", normed, split_weight, preferred_element_type=jnp.float32
    )
    total_rows = projected.shape[2]
    head_q = (projected[0] + split_bias[0]).astype(jnp.bfloat16)
    head_k = (projected[1] + split_bias[1]).astype(jnp.bfloat16)
    head_v = (projected[2] + split_bias[2]).astype(jnp.bfloat16)
    scores = jnp.einsum(
        "hqe,hke->hqk", head_q, head_k, preferred_element_type=jnp.float32
    ) * HEAD_DIM ** (-0.5)
    pieces = prompt_pieces[0]
    position = jnp.arange(total_rows)
    allowed = (pieces[:, None] == pieces[None, :]) & (position[None, :] <= position[:, None])
    scores = jnp.where(allowed[None], scores, -1e30)
    highest = jnp.max(scores, axis=-1, keepdims=True)
    weights = jnp.exp(scores - highest)
    probs = (weights / jnp.sum(weights, axis=-1, keepdims=True)).astype(jnp.bfloat16)
    context = jnp.einsum("hqk,hke->qhe", probs, head_v, preferred_element_type=jnp.float32)
    context = context.reshape(total_rows, width).astype(jnp.bfloat16)
    key_rows = jnp.transpose(head_k, (1, 0, 2)).reshape(total_rows, width)
    value_rows = jnp.transpose(head_v, (1, 0, 2)).reshape(total_rows, width)
    prompt_partial = jnp.dot(context, out_weight, preferred_element_type=jnp.float32).astype(
        jnp.bfloat16
    )
    prompt_partial, own_out, key_rows, value_rows, key_new, value_new = lax.optimization_barrier(
        (prompt_partial, own_out, key_rows, value_rows, key_new, value_new)
    )
    written = (jnp.arange(past_cache.shape[2])[None, :] == request_ages[:staying, None])
    fresh = jnp.stack([key_new[:staying], value_new[:staying]], axis=1)
    kept_cache = jnp.where(
        written[:, None, :, None], fresh[:, :, None, :], past_cache[:staying]
    )
    attended = lax.psum_scatter(prompt_partial, "tp", scatter_dimension=0, tiled=True).astype(
        jnp.float32
    )
    own_out, kept_cache = lax.optimization_barrier((own_out, kept_cache))
    decode_out = gather_over_tp(own_out)
    prompt_out = (prompt_rows.astype(jnp.float32) + attended + out_bias).astype(jnp.bfloat16)
    prompt_cache = jnp.stack([key_rows, value_rows])
    kept_out = decode_out[:staying]
    send_rows = jnp.where(has[:, None], decode_out[picks], jnp.zeros((), jnp.bfloat16))
    send_rows, moved_cache = lax.optimization_barrier((send_rows, moved_cache))
    moved_cache = jnp.where(request_ages[0] > 0, moved_cache, jnp.zeros((), jnp.bfloat16))
    moved_out = lax.all_to_all(send_rows, "rep", split_axis=0, concat_axis=0, tiled=True)
    return (prompt_out, prompt_cache, kept_out, kept_cache, moved_out, moved_cache)


def solution(mesh):
    placed = (
        P(("rep", "tp"), None),
        P("rep", None),
        P("rep", None),
        P("rep"),
        P("rep", None),
        P("rep", None, None, "tp"),
        P(),
        P(),
        P(None, None, "tp"),
        P(None, "tp"),
        P("tp", None),
        P(),
    )
    return jax.shard_map(
        on_device,
        mesh=mesh,
        in_specs=placed,
        out_specs=(
            P(("rep", "tp"), None),
            P(None, "rep", "tp"),
            P("rep", None),
            P("rep", None, None, "tp"),
            P("rep", None),
            P("rep", None, None, "tp"),
        ),
        check_vma=False,
    )
```

```python
import jax
import jax.numpy as jnp
from jax import lax
from jax.sharding import PartitionSpec as P

HEAD_DIM = 128
CAP = 1


EPSILON = 1e-05


def layer_norm(values, norm_gain, norm_bias):
    wide = values.astype(jnp.float32)
    center = jnp.mean(wide, axis=-1, keepdims=True)
    spread = jnp.mean(jnp.square(wide - center), axis=-1, keepdims=True)
    scaled = (wide - center) * lax.rsqrt(spread + EPSILON)
    return (scaled * norm_gain + norm_bias).astype(jnp.bfloat16)


def decode_project(rows, norm_gain, norm_bias, qkv_weight, qkv_bias):
    normed = layer_norm(rows, norm_gain, norm_bias)
    projected = jnp.einsum("rd,cde->cre", normed, qkv_weight, preferred_element_type=jnp.float32)
    return tuple((projected[i] + qkv_bias[i]).astype(jnp.bfloat16) for i in range(3))


def decode_partial(queries, key_new, value_new, cache, ages, out_weight):
    count = queries.shape[0]
    width = queries.shape[1]
    heads_here = width // HEAD_DIM
    length = cache.shape[2]
    head_of_col = jnp.arange(width) // HEAD_DIM
    diag = jnp.arange(heads_here)[:, None] == head_of_col[None, :]
    q_blocks = jnp.where(diag[None], queries[:, None, :], jnp.zeros((), jnp.bfloat16))
    scale = HEAD_DIM ** (-0.5)
    scores = (
        jnp.einsum("rhc,rlc->rhl", q_blocks, cache[:, 0], preferred_element_type=jnp.float32)
        * scale
    )
    own = (
        jnp.sum(
            (queries.astype(jnp.float32) * key_new.astype(jnp.float32)).reshape(
                count, heads_here, HEAD_DIM
            ),
            axis=-1,
        )
        * scale
    )
    live = jnp.arange(length)[None, :] < ages[:, None]
    scores = jnp.where(live[:, None, :], scores, -1e30)
    highest = jnp.maximum(jnp.max(scores, axis=-1), own)
    weights = jnp.exp(scores - highest[..., None])
    own_weight = jnp.exp(own - highest)
    total = jnp.sum(weights, axis=-1) + own_weight
    probs = (weights / total[..., None]).astype(jnp.bfloat16)
    own_prob = (own_weight / total).astype(jnp.bfloat16)
    mixed = jnp.einsum("rhl,rlc->rhc", probs, cache[:, 1], preferred_element_type=jnp.float32)
    context = jnp.sum(jnp.where(diag[None], mixed, 0.0), axis=1)
    context = context + own_prob.astype(jnp.float32)[:, head_of_col] * value_new.astype(jnp.float32)
    context = context.astype(jnp.bfloat16)
    partial_value = jnp.dot(context, out_weight, preferred_element_type=jnp.float32)
    return partial_value


def updated_rows(cache, key_new, value_new, ages, picks):
    length = cache.shape[2]
    fresh = jnp.stack([key_new, value_new], axis=1)[picks]
    written = jnp.arange(length)[None, :] == ages[picks][:, None]
    return jnp.where(written[:, None, :, None], fresh[:, :, None, :], cache[picks])


def scatter_over_tp(pieces, rows, out_bias):
    n = lax.axis_size("tp")
    me = lax.axis_index("tp")
    share = pieces.shape[1]
    rolled = jnp.take(pieces, (me + jnp.arange(n)) % n, axis=0)
    total = rolled[0].astype(jnp.float32)
    for shift in range(1, n):
        got = lax.ppermute(rolled[shift], "tp", [(i, (i + shift) % n) for i in range(n)])
        total = total + got.astype(jnp.float32)
    own_rows = lax.dynamic_slice_in_dim(rows, me * share, share, 0)
    return (own_rows.astype(jnp.float32) + total + out_bias).astype(jnp.bfloat16)


def gather_over_tp(own_out):
    n = lax.axis_size("tp")
    me = lax.axis_index("tp")
    held = [own_out]
    for shift in range(1, n):
        held.append(lax.ppermute(own_out, "tp", [(i, (i + shift) % n) for i in range(n)]))
    stacked = jnp.stack(held)
    return jnp.take(stacked, (me - jnp.arange(n)) % n, axis=0).reshape(-1, own_out.shape[1])


def on_device(
    prompt_rows,
    prompt_pieces,
    decode_rows,
    request_ages,
    migrate_to,
    past_cache,
    norm_gain,
    norm_bias,
    qkv_weight,
    qkv_bias,
    out_weight,
    out_bias,
):
    rep_count = lax.axis_size("rep")
    width = qkv_weight.shape[2]
    heads_here = width // HEAD_DIM
    leaving = migrate_to.shape[0]
    staying = decode_rows.shape[0] - leaving
    targets = migrate_to[:, 0]
    match = targets[None, :] == jnp.arange(rep_count * CAP)[:, None]
    has = jnp.any(match, axis=1)
    picks = staying + jnp.sum(jnp.where(match, jnp.arange(leaving)[None, :], 0), axis=1)
    queries_new, key_new, value_new = decode_project(
        decode_rows, norm_gain, norm_bias, qkv_weight, qkv_bias
    )
    leave_written = jnp.arange(past_cache.shape[2])[None, :] == request_ages[staying:, None]
    leave_fresh = jnp.stack([key_new[staying:], value_new[staying:]], axis=1)
    leave_rows = jnp.where(
        leave_written[:, None, :, None], leave_fresh[:, :, None, :], past_cache[staying:]
    )
    padded = jnp.concatenate([leave_rows, jnp.zeros_like(leave_rows[:1])], axis=0)
    send_cache = padded[jnp.where(has, picks - staying, leaving)]
    send_cache, attend_cache = lax.optimization_barrier((send_cache, past_cache))
    moved_cache = lax.all_to_all(send_cache, "rep", split_axis=0, concat_axis=0, tiled=True)
    partial_value = decode_partial(
        queries_new, key_new, value_new, attend_cache, request_ages, out_weight
    )
    tp_count = lax.axis_size("tp")
    decode_pieces = partial_value.astype(jnp.bfloat16).reshape(
        tp_count, decode_rows.shape[0] // tp_count, decode_rows.shape[1]
    )
    own_out = scatter_over_tp(decode_pieces, decode_rows, out_bias)
    normed = lax.all_gather(layer_norm(prompt_rows, norm_gain, norm_bias), "tp", axis=0, tiled=True)
    projected = jnp.einsum("rd,cde->cre", normed, qkv_weight, preferred_element_type=jnp.float32)
    total_rows = projected.shape[1]
    queries = (projected[0] + qkv_bias[0]).astype(jnp.bfloat16)
    key_rows = (projected[1] + qkv_bias[1]).astype(jnp.bfloat16)
    value_rows = (projected[2] + qkv_bias[2]).astype(jnp.bfloat16)
    diag = jnp.arange(heads_here)[:, None] == (jnp.arange(width) // HEAD_DIM)[None, :]
    q_blocks = jnp.where(diag[:, None, :], queries[None], jnp.zeros((), jnp.bfloat16))
    scores = jnp.einsum(
        "hqc,kc->hqk", q_blocks, key_rows, preferred_element_type=jnp.float32
    ) * HEAD_DIM ** (-0.5)
    pieces = prompt_pieces[0]
    position = jnp.arange(total_rows)
    allowed = (pieces[:, None] == pieces[None, :]) & (position[None, :] <= position[:, None])
    scores = jnp.where(allowed[None], scores, -1e30)
    highest = jnp.max(scores, axis=-1, keepdims=True)
    weights = jnp.exp(scores - highest)
    probs = (weights / jnp.sum(weights, axis=-1, keepdims=True)).astype(jnp.bfloat16)
    mixed = jnp.einsum("hqk,kc->hqc", probs, value_rows, preferred_element_type=jnp.float32)
    context = jnp.sum(jnp.where(diag[:, None, :], mixed, 0.0), axis=0).astype(jnp.bfloat16)
    prompt_partial = jnp.dot(context, out_weight, preferred_element_type=jnp.float32).astype(
        jnp.bfloat16
    )
    prompt_partial, own_out, key_rows, value_rows, key_new, value_new = lax.optimization_barrier(
        (prompt_partial, own_out, key_rows, value_rows, key_new, value_new)
    )
    written = (jnp.arange(past_cache.shape[2])[None, :] == request_ages[:staying, None])
    fresh = jnp.stack([key_new[:staying], value_new[:staying]], axis=1)
    kept_cache = jnp.where(
        written[:, None, :, None], fresh[:, :, None, :], past_cache[:staying]
    )
    attended = lax.psum_scatter(prompt_partial, "tp", scatter_dimension=0, tiled=True).astype(
        jnp.float32
    )
    own_out, kept_cache = lax.optimization_barrier((own_out, kept_cache))
    decode_out = gather_over_tp(own_out)
    prompt_out = (prompt_rows.astype(jnp.float32) + attended + out_bias).astype(jnp.bfloat16)
    prompt_cache = jnp.stack([key_rows, value_rows])
    kept_out = decode_out[:staying]
    send_rows = jnp.where(has[:, None], decode_out[picks], jnp.zeros((), jnp.bfloat16))
    send_rows, moved_cache = lax.optimization_barrier((send_rows, moved_cache))
    moved_cache = jnp.where(request_ages[0] > 0, moved_cache, jnp.zeros((), jnp.bfloat16))
    moved_out = lax.all_to_all(send_rows, "rep", split_axis=0, concat_axis=0, tiled=True)
    return (prompt_out, prompt_cache, kept_out, kept_cache, moved_out, moved_cache)


def solution(mesh):
    placed = (
        P(("rep", "tp"), None),
        P("rep", None),
        P("rep", None),
        P("rep"),
        P("rep", None),
        P("rep", None, None, "tp"),
        P(),
        P(),
        P(None, None, "tp"),
        P(None, "tp"),
        P("tp", None),
        P(),
    )
    return jax.shard_map(
        on_device,
        mesh=mesh,
        in_specs=placed,
        out_specs=(
            P(("rep", "tp"), None),
            P(None, "rep", "tp"),
            P("rep", None),
            P("rep", None, None, "tp"),
            P("rep", None),
            P("rep", None, None, "tp"),
        ),
        check_vma=False,
    )
```
